128 devices in a mesh: blk: 32 (over z, y, core), tp: 4 (over x).
Axes of the slice: x: 4, y: 4, z: 4, core: 2. Of those that a mesh axis runs over, the one named last changes fastest.
Arguments:
- tokens: bfloat16 [16384, 1664], P('blk', 'tp'), may hold values from -8 to 8
- block_split: int32 [64], replicated, may hold values from 0 to 63, each once
- req_lengths: int32 [128], replicated, may hold values from 1 to 125, as said below
- req_owners: int32 [128], replicated, may hold values from 0 to 31, as said below
- norm1_gain: float32 [1664], replicated, may hold values from 0.25 to 1.75
- qkv_weight: bfloat16 [1664, 3, 1664], P(None, None, 'tp'), may hold values from -2 to 2
- out_weight: bfloat16 [1664, 1664], P('tp'), may hold values from -0.15625 to 0.15625
- norm2_gain: float32 [1664], replicated, may hold values from 0.25 to 1.75
- up_weight: bfloat16 [1664, 8192], P(None, 'tp'), may hold values from -0.15625 to 0.15625
- down_weight: bfloat16 [8192, 1664], P('tp'), may hold values from -0.0625 to 0.0625
- merge_gain: float32 [1664], replicated, may hold values from 0.25 to 1.75
- merge_weight: bfloat16 [6656, 1664], P(None, 'tp'), may hold values from -0.078125 to 0.078125
Outputs:
- returned: bfloat16 [4096, 1664], P('blk', 'tp')
The draws below stay inside these ranges and needn't reach their ends.
Inputs may be any that keep to these rules, and one draw needn't show every extreme that they name: Index d of blk holds packed blocks block_split[2d] and block_split[2d + 1], each of 256 tokens; every block once. `req_lengths`: lengths count merge groups of 4 tokens; the requests of each owner add up to exactly 128 groups. `req_owners`: every owner index holds exactly 4 requests.
All inputs are finite; a program needn't handle non-finite values.
Results may differ from the reference program's by a relative error of at most 0.015.
Values may be sent and summed in bfloat16 or wider, within the bound.
No kernel may reach another device: no remote copies, remote signals or barrier semaphores. Data moves between devices by JAX's collectives and lax.ppermute only.
A program may use at most 128 MiB of HBM per device.

```python
import jax
import jax.numpy as jnp
from jax import lax

D = 1664
HEADS = 16
FF = 8192
HDIM = 104
TOK_DEV = 512
REQ_OWN = 4
GROUP_DEV = 128
TOKENS = 16384
NREQ = 128
MERGED = 4096
N_BLK = 32
N_TP = 4


def request_plan(key):
    plan_key = jax.random.fold_in(key, 11)
    owner_total = NREQ // REQ_OWN

    def one_owner(owner_index):
        owner_key = jax.random.fold_in(plan_key, owner_index)
        random_cuts = jax.random.permutation(owner_key, GROUP_DEV - 1)[:REQ_OWN - 1] + 1
        fixed_cuts = jnp.arange(1, REQ_OWN, dtype=jnp.int32)
        cut_points = jnp.where(owner_index == 0, fixed_cuts, random_cuts.astype(jnp.int32))
        cut_points = jnp.sort(cut_points.astype(jnp.int32))
        bounds = jnp.concatenate([jnp.zeros((1,), jnp.int32), cut_points, jnp.full((1,), GROUP_DEV, jnp.int32)])
        return bounds[1:] - bounds[:-1]
    owner_sizes = jax.vmap(one_owner)(jnp.arange(owner_total, dtype=jnp.int32))
    pack_order = jax.random.permutation(jax.random.fold_in(plan_key, 99991), NREQ)
    flat_sizes = owner_sizes.reshape(-1)[pack_order]
    flat_owners = (jnp.arange(NREQ, dtype=jnp.int32) // REQ_OWN)[pack_order]
    return (flat_sizes.astype(jnp.int32), flat_owners.astype(jnp.int32))


def draw_req_lengths(key, part):
    return request_plan(key)[0]


def draw_req_owners(key, part):
    return request_plan(key)[1]


def draw_tokens(key, part):
    normal_key = jax.random.fold_in(key, 0)
    sampled = jax.random.normal(normal_key, (TOKENS, D), jnp.float32)
    return jnp.clip(sampled, -8.0, 8.0).astype(jnp.bfloat16)


def draw_qkv_weight(key, part):
    sampled = jax.random.normal(key, (D, 3, D), jnp.float32) * D ** (-0.5)
    return jnp.clip(sampled, -2.0, 2.0).astype(jnp.bfloat16)


def block_levels(stream_key, shape, shards, low, high):
    level, own = 1.0, jax.random.fold_in(stream_key, 6)
    for dim, shards_of in shards:
        steps = jnp.exp(jax.random.uniform(jax.random.fold_in(own, dim), (shards_of,), jnp.float32, low / len(shards), high / len(shards)))
        level = level * jnp.repeat(steps, shape[dim] // shards_of).reshape([-1 if axis == dim else 1 for axis in range(len(shape))])
    return level


def scatter_about(own_key, shape, scale, limit, shards=(), kind=jnp.bfloat16):
    values = scale * jax.random.normal(own_key, shape, jnp.float32)
    if shards:
        values = values * block_levels(own_key, shape, shards, -0.22, 0.18)
    return jnp.clip(values, -limit, limit).astype(kind)


def setup_inputs(seed: int = 0) -> dict:
    key_list = jax.random.split(jax.random.key(seed), 13)
    return {
        "tokens": draw_tokens(jax.random.fold_in(key_list[12], 71), 0),
        "block_split": jax.random.permutation(key_list[1], 2 * N_BLK).astype(jnp.int32),
        "req_lengths": draw_req_lengths(jax.random.fold_in(key_list[12], 71), 0),
        "req_owners": draw_req_owners(jax.random.fold_in(key_list[12], 71), 0),
        "norm1_gain": jnp.clip(1.0 + 0.15 * jax.random.normal(key_list[4], (D,), jnp.float32), 0.25, 1.75),
        "qkv_weight": draw_qkv_weight(jax.random.fold_in(key_list[12], 71), 0),
        "out_weight": scatter_about(key_list[6], (D, D), D ** -0.5, 0.15625, ((0, 4),)),
        "norm2_gain": jnp.clip(1.0 + 0.15 * jax.random.normal(key_list[7], (D,), jnp.float32), 0.25, 1.75),
        "up_weight": scatter_about(key_list[8], (D, FF), D ** -0.5, 0.15625, ((1, 4),)),
        "down_weight": scatter_about(key_list[9], (FF, D), FF ** -0.5, 0.0625, ((0, 4),)),
        "merge_gain": jnp.clip(1.0 + 0.15 * jax.random.normal(key_list[10], (D,), jnp.float32), 0.25, 1.75),
        "merge_weight": scatter_about(key_list[11], (4 * D, D), (4 * D) ** -0.5, 0.078125, ((1, 4),)),
    }


EPSILON = 1e-06
MASKED = -1e+30

def layer_norm(values, norm_gain):
    values = values.astype(jnp.float32)
    row_mean = lax.optimization_barrier(jnp.mean(values, axis=-1, keepdims=True))
    centred = values - row_mean
    spread = lax.optimization_barrier(jnp.mean(centred * centred, axis=-1, keepdims=True))
    return centred * lax.rsqrt(spread + EPSILON) * norm_gain

def request_tables(req_lengths, req_owners):
    request_ends = jnp.cumsum(req_lengths).astype(jnp.int32)
    starts = request_ends - req_lengths
    position = jnp.arange(req_lengths.shape[0], dtype=jnp.int32)
    earlier = (req_owners[None, :] == req_owners[:, None]) & (position[None, :] < position[:, None])
    owner_offset = lax.optimization_barrier(jnp.sum(jnp.where(earlier, req_lengths[None, :], 0), axis=1)).astype(jnp.int32)
    return (starts, request_ends, owner_offset)

def attend(carried, query_rows, query_seg, key_rows, value_rows, key_seg):
    maxima, totals, accumulated = carried
    query_count = query_rows.shape[0]
    key_count = key_rows.shape[0]
    head_count = accumulated.shape[1]
    head_size = accumulated.shape[2]
    query_heads = query_rows.reshape(query_count, head_count, head_size).astype(jnp.float32)
    key_heads = key_rows.reshape(key_count, head_count, head_size).astype(jnp.float32)
    value_heads = value_rows.reshape(key_count, head_count, head_size).astype(jnp.float32)
    scores = jnp.einsum('qhd,khd->hqk', query_heads, key_heads) * head_size ** (-0.5)
    same_request = (query_seg[:, None] == key_seg[None, :])[None, :, :]
    scores = jnp.where(same_request, scores, MASKED)
    new_max = jnp.maximum(maxima, lax.optimization_barrier(jnp.max(scores, axis=2)))
    weights = jnp.where(same_request, jnp.exp(scores - new_max[:, :, None]), 0.0)
    factor = jnp.exp(maxima - new_max)
    totals = totals * factor + lax.optimization_barrier(jnp.sum(weights, axis=2))
    mixed_values = jnp.einsum('hqk,khd->qhd', weights.astype(jnp.bfloat16).astype(jnp.float32), value_heads)
    accumulated = accumulated * jnp.transpose(factor)[:, :, None] + mixed_values
    return (new_max, totals, accumulated)

def split_sum(left, right, groups):
    group_width = left.shape[1] // groups
    total_sum = jnp.zeros((left.shape[0], right.shape[1]), jnp.float32)
    for group_index in range(groups):
        term = jnp.dot(left[:, group_index * group_width:(group_index + 1) * group_width], right[group_index * group_width:(group_index + 1) * group_width], preferred_element_type=jnp.float32)
        rounded = lax.optimization_barrier(term.astype(jnp.bfloat16))
        total_sum = total_sum + rounded.astype(jnp.float32)
    return total_sum

def reference(tokens, block_split, req_lengths, req_owners, norm1_gain, qkv_weight, out_weight, norm2_gain, up_weight, down_weight, merge_gain, merge_weight):
    half_rows = TOK_DEV // 2
    starts, request_ends, owner_offset = request_tables(req_lengths, req_owners)
    places = jnp.arange(2 * N_BLK, dtype=jnp.int32)
    packed_index = jnp.arange(TOKENS, dtype=jnp.int32)
    packed_block = packed_index // half_rows
    held_at = lax.optimization_barrier(jnp.sum(jnp.where(block_split[None, :] == packed_block[:, None], places[None, :], 0), axis=1)).astype(jnp.int32)
    packed = jnp.take(tokens, held_at * half_rows + packed_index % half_rows, axis=0)
    segment = lax.optimization_barrier(jnp.sum((request_ends[None, :] <= (packed_index // 4)[:, None]).astype(jnp.int32), axis=1)).astype(jnp.int32)
    normed1 = layer_norm(packed, norm1_gain).astype(jnp.bfloat16)
    projected = jnp.einsum('td,dcf->ctf', normed1.astype(jnp.float32), qkv_weight.astype(jnp.float32)).astype(jnp.bfloat16)
    pad_rows = jnp.zeros((TOK_DEV, D), jnp.bfloat16)
    key_pad = jnp.concatenate([pad_rows, projected[1], pad_rows], axis=0)
    value_pad = jnp.concatenate([pad_rows, projected[2], pad_rows], axis=0)
    seg_rim = jnp.full((TOK_DEV,), -1, jnp.int32)
    seg_pad = jnp.concatenate([seg_rim, segment, seg_rim], axis=0)
    queries = projected[0]

    def one_block(block_index):
        row_start = block_index * TOK_DEV
        query_rows = lax.dynamic_slice_in_dim(queries, row_start, TOK_DEV, 0)
        query_seg = lax.dynamic_slice_in_dim(segment, row_start, TOK_DEV, 0)
        key_rows = lax.dynamic_slice_in_dim(key_pad, row_start, 3 * TOK_DEV, 0)
        value_rows = lax.dynamic_slice_in_dim(value_pad, row_start, 3 * TOK_DEV, 0)
        key_seg = lax.dynamic_slice_in_dim(seg_pad, row_start, 3 * TOK_DEV, 0)
        start_state = (jnp.full((HEADS, TOK_DEV), MASKED, jnp.float32), jnp.zeros((HEADS, TOK_DEV), jnp.float32), jnp.zeros((TOK_DEV, HEADS, HDIM), jnp.float32))
        maxima, totals, accumulated = attend(start_state, query_rows, query_seg, key_rows, value_rows, key_seg)
        return (accumulated / jnp.transpose(totals)[:, :, None]).reshape(TOK_DEV, D).astype(jnp.bfloat16)
    attended = lax.map(one_block, jnp.arange(N_BLK, dtype=jnp.int32)).reshape(TOKENS, D)
    after_attention = packed.astype(jnp.float32) + split_sum(attended, out_weight, N_TP)
    normed2 = layer_norm(after_attention, norm2_gain).astype(jnp.bfloat16)
    hidden = jax.nn.gelu(jnp.dot(normed2, up_weight, preferred_element_type=jnp.float32), approximate=False).astype(jnp.bfloat16)
    after_mlp = after_attention + split_sum(hidden, down_weight, N_TP)
    final_norm = layer_norm(after_mlp, merge_gain).astype(jnp.bfloat16)
    merged = jnp.dot(final_norm.reshape(MERGED, 4 * D), merge_weight, preferred_element_type=jnp.float32).astype(jnp.bfloat16)
    group_index = jnp.arange(MERGED, dtype=jnp.int32)
    request = lax.optimization_barrier(jnp.sum((request_ends[None, :] <= group_index[:, None]).astype(jnp.int32), axis=1)).astype(jnp.int32)
    chosen = request[:, None] == jnp.arange(NREQ, dtype=jnp.int32)[None, :]
    target = lax.optimization_barrier(jnp.sum(jnp.where(chosen, (req_owners * GROUP_DEV + owner_offset - starts)[None, :], 0), axis=1)).astype(jnp.int32) + group_index
    return jnp.zeros_like(merged).at[target].set(merged)
```

```python
import jax
import jax.numpy as jnp
from jax import lax
from jax.sharding import PartitionSpec as P

HDIM = 104


EPSILON = 1e-06
MASKED = -1e30


def layer_norm(values, norm_gain):
    values = values.astype(jnp.float32)
    row_mean = jnp.mean(values, axis=-1, keepdims=True)
    centred = values - row_mean
    spread = jnp.mean(centred * centred, axis=-1, keepdims=True)
    return centred * lax.rsqrt(spread + EPSILON) * norm_gain


def segment_at(positions, request_ends):
    return jnp.sum((request_ends[None, :] <= (positions // 4)[:, None]).astype(jnp.int32), axis=1)


def make_body(n_blk):
    def body(
        tokens,
        block_split,
        req_lengths,
        req_owners,
        norm1_gain,
        qkv_weight,
        out_weight,
        norm2_gain,
        up_weight,
        down_weight,
        merge_gain,
        merge_weight,
    ):
        tok_rows, width = tokens.shape
        half_rows = tok_rows // 2
        piece = half_rows // n_blk
        n_slots = block_split.shape[0]
        my_index = lax.axis_index("blk")

        slots = jnp.arange(n_slots, dtype=jnp.int32)
        inverse = jnp.sum(
            jnp.where(block_split[None, :] == slots[:, None], slots[None, :], 0), axis=1
        )
        spread = tokens.reshape(2, n_blk, piece, width).transpose(1, 0, 2, 3)
        spread = lax.all_to_all(spread, "blk", 0, 0, tiled=True)
        spread = spread.reshape(n_slots, piece, width)
        routed = jnp.take(spread, inverse, axis=0).reshape(n_blk, 2, piece, width)
        routed = lax.all_to_all(routed, "blk", 0, 0, tiled=True)
        local = routed.transpose(1, 0, 2, 3).reshape(tok_rows, width)

        request_ends = jnp.cumsum(req_lengths).astype(jnp.int32)
        starts = request_ends - req_lengths
        row_base = my_index * tok_rows
        query_seg = segment_at(row_base + jnp.arange(tok_rows, dtype=jnp.int32), request_ends)
        key_pos = row_base - tok_rows + jnp.arange(3 * tok_rows, dtype=jnp.int32)
        key_valid = (key_pos >= 0) & (key_pos < n_blk * tok_rows)
        key_seg = jnp.where(key_valid, segment_at(key_pos, request_ends), -1)

        features = lax.all_gather(local, "tp", axis=1, tiled=True)
        normed1 = layer_norm(features, norm1_gain).astype(jnp.bfloat16)
        projected = jnp.einsum(
            "td,dcf->ctf", normed1, qkv_weight, preferred_element_type=jnp.float32
        ).astype(jnp.bfloat16)
        queries = projected[0]
        key_value = projected[1:]
        from_prev = lax.ppermute(key_value, "blk", [(i, i + 1) for i in range(n_blk - 1)])
        from_next = lax.ppermute(key_value, "blk", [(i + 1, i) for i in range(n_blk - 1)])
        window = jnp.concatenate([from_prev, key_value, from_next], axis=1)

        head_count = qkv_weight.shape[2] // HDIM
        query_heads = queries.reshape(tok_rows, head_count, HDIM)
        key_heads = window[0].reshape(3 * tok_rows, head_count, HDIM)
        value_heads = window[1].reshape(3 * tok_rows, head_count, HDIM)
        scores = jnp.einsum(
            "qhd,khd->hqk", query_heads, key_heads, preferred_element_type=jnp.float32
        ) * HDIM ** (-0.5)
        same_request = (query_seg[:, None] == key_seg[None, :])[None, :, :]
        scores = jnp.where(same_request, scores, MASKED)
        maxima = jnp.max(scores, axis=2)
        weights = jnp.where(same_request, jnp.exp(scores - maxima[:, :, None]), 0.0)
        totals = jnp.sum(weights, axis=2)
        mixed = jnp.einsum(
            "hqk,khd->qhd",
            weights.astype(jnp.bfloat16),
            value_heads,
            preferred_element_type=jnp.float32,
        )
        attended = (mixed / jnp.transpose(totals)[:, :, None]).reshape(tok_rows, -1).astype(
            jnp.bfloat16
        )

        residual = features.astype(jnp.float32)
        after_attention = residual + lax.psum(
            jnp.dot(attended, out_weight, preferred_element_type=jnp.float32).astype(jnp.bfloat16),
            "tp",
        ).astype(jnp.float32)
        normed2 = layer_norm(after_attention, norm2_gain).astype(jnp.bfloat16)
        hidden = jax.nn.gelu(
            jnp.dot(normed2, up_weight, preferred_element_type=jnp.float32), approximate=False
        ).astype(jnp.bfloat16)
        after_mlp = after_attention + lax.psum(
            jnp.dot(hidden, down_weight, preferred_element_type=jnp.float32).astype(jnp.bfloat16),
            "tp",
        ).astype(jnp.float32)
        final_norm = layer_norm(after_mlp, merge_gain).astype(jnp.bfloat16)
        group_rows = tok_rows // 4
        grouped = final_norm.reshape(group_rows, 4 * final_norm.shape[1])
        merged = jnp.dot(grouped, merge_weight, preferred_element_type=jnp.float32).astype(
            jnp.bfloat16
        )
        out_width = merged.shape[1]

        all_groups = jnp.arange(n_blk * group_rows, dtype=jnp.int32)
        request = jnp.sum((request_ends[None, :] <= all_groups[:, None]).astype(jnp.int32), axis=1)
        position = jnp.arange(req_lengths.shape[0], dtype=jnp.int32)
        earlier = (req_owners[None, :] == req_owners[:, None]) & (position[None, :] < position[:, None])
        owner_offset = jnp.sum(jnp.where(earlier, req_lengths[None, :], 0), axis=1)
        shift = req_owners * group_rows + owner_offset - starts
        target = jnp.take(shift, request) + all_groups
        dest = target // group_rows

        rounds = group_rows // n_blk
        spread_m = merged.reshape(rounds, n_blk, out_width).transpose(1, 0, 2)
        spread_m = lax.all_to_all(spread_m, "blk", 0, 0, tiled=True)
        spread_m = spread_m.reshape(n_blk * rounds, out_width)
        held_local = jnp.arange(n_blk * rounds, dtype=jnp.int32)
        held_group = (held_local // rounds) * group_rows + (held_local % rounds) * n_blk + my_index
        held_dest = jnp.take(dest, held_group)
        same_dest = held_dest[:, None] == held_dest[None, :]
        before = held_local[None, :] < held_local[:, None]
        held_rank = jnp.sum((same_dest & before).astype(jnp.int32), axis=1)
        capacity = 8
        dest_ids = jnp.arange(n_blk, dtype=jnp.int32)
        cells = jnp.arange(capacity, dtype=jnp.int32)
        hit = (held_dest[None, None, :] == dest_ids[:, None, None]) & (
            held_rank[None, None, :] == cells[None, :, None]
        )
        send_index = jnp.sum(jnp.where(hit, held_local[None, None, :], 0), axis=2)
        send = jnp.take(spread_m, send_index.reshape(-1), axis=0).reshape(n_blk, capacity, out_width)
        received = lax.all_to_all(send, "blk", 0, 0, tiled=True).reshape(n_blk * capacity, out_width)

        my_slots = my_index * group_rows + jnp.arange(group_rows, dtype=jnp.int32)
        source = jnp.sum(
            jnp.where(target[None, :] == my_slots[:, None], all_groups[None, :], 0), axis=1
        )
        source_dev = source % n_blk
        same_src = source_dev[:, None] == source_dev[None, :]
        earlier_src = source[None, :] < source[:, None]
        cell = jnp.sum((same_src & earlier_src).astype(jnp.int32), axis=1)
        return jnp.take(received, source_dev * capacity + cell, axis=0)

    return body


def solution(mesh):
    n_blk = mesh.shape["blk"]
    return jax.shard_map(
        make_body(n_blk),
        mesh=mesh,
        in_specs=(
            P("blk", "tp"),
            P(),
            P(),
            P(),
            P(),
            P(None, None, "tp"),
            P("tp", None),
            P(),
            P(None, "tp"),
            P("tp", None),
            P(),
            P(None, "tp"),
        ),
        out_specs=P("blk", "tp"),
        check_vma=False,
    )
```

```python
import jax
import jax.numpy as jnp
from jax import lax
from jax.sharding import PartitionSpec as P

HDIM = 104


EPSILON = 1e-06
MASKED = -1e30


def layer_norm(values, norm_gain):
    values = values.astype(jnp.float32)
    row_mean = jnp.mean(values, axis=-1, keepdims=True)
    centred = values - row_mean
    spread = jnp.mean(centred * centred, axis=-1, keepdims=True)
    return centred * lax.rsqrt(spread + EPSILON) * norm_gain


def segment_at(positions, request_ends):
    return jnp.sum((request_ends[None, :] <= (positions // 4)[:, None]).astype(jnp.int32), axis=1)


def tp_gather_rows(chunk, n_tp):
    me = lax.axis_index("tp")
    full = jnp.zeros((n_tp,) + chunk.shape, chunk.dtype)
    full = lax.dynamic_update_index_in_dim(full, chunk, me, 0)
    for step in range(1, n_tp):
        got = lax.ppermute(chunk, "tp", [(i, (i + step) % n_tp) for i in range(n_tp)])
        full = lax.dynamic_update_index_in_dim(full, got, (me - step) % n_tp, 0)
    return full


def tp_scatter_sum(partial, n_tp):
    me = lax.axis_index("tp")
    chunks = partial.reshape((n_tp, partial.shape[0] // n_tp) + partial.shape[1:])
    total = lax.dynamic_index_in_dim(chunks, me, 0, keepdims=False).astype(jnp.float32)
    for step in range(1, n_tp):
        send = lax.dynamic_index_in_dim(chunks, (me + step) % n_tp, 0, keepdims=False)
        got = lax.ppermute(send, "tp", [(i, (i + step) % n_tp) for i in range(n_tp)])
        total = total + got.astype(jnp.float32)
    return total


def make_body(n_blk, n_tp):
    def body(
        tokens,
        block_split,
        req_lengths,
        req_owners,
        norm1_gain,
        qkv_weight,
        out_weight,
        norm2_gain,
        up_weight,
        down_weight,
        merge_gain,
        merge_weight,
    ):
        tok_rows, width = tokens.shape
        half_rows = tok_rows // 2
        piece = half_rows // n_blk
        n_slots = block_split.shape[0]
        my_index = lax.axis_index("blk")

        slots = jnp.arange(n_slots, dtype=jnp.int32)
        inverse = jnp.sum(
            jnp.where(block_split[None, :] == slots[:, None], slots[None, :], 0), axis=1
        )
        spread = tokens.reshape(2, n_blk, piece, width).transpose(1, 0, 2, 3)
        spread = lax.all_to_all(spread, "blk", 0, 0, tiled=True)
        spread = spread.reshape(n_slots, piece, width)
        routed = jnp.take(spread, inverse, axis=0).reshape(n_blk, 2, piece, width)
        routed = lax.all_to_all(routed, "blk", 0, 0, tiled=True)
        local = routed.transpose(1, 0, 2, 3).reshape(tok_rows, width)

        request_ends = jnp.cumsum(req_lengths).astype(jnp.int32)
        starts = request_ends - req_lengths
        row_base = my_index * tok_rows
        query_seg = segment_at(row_base + jnp.arange(tok_rows, dtype=jnp.int32), request_ends)
        key_pos = row_base - tok_rows + jnp.arange(3 * tok_rows, dtype=jnp.int32)
        key_valid = (key_pos >= 0) & (key_pos < n_blk * tok_rows)
        key_seg = jnp.where(key_valid, segment_at(key_pos, request_ends), -1)

        stacked = tp_gather_rows(local, n_tp)
        features = stacked.transpose(1, 0, 2).reshape(tok_rows, n_tp * width)
        normed1 = layer_norm(features, norm1_gain).astype(jnp.bfloat16)
        projected = jnp.einsum(
            "td,dcf->ctf", normed1, qkv_weight, preferred_element_type=jnp.float32
        ).astype(jnp.bfloat16)
        queries = projected[0]
        key_value = projected[1:]
        from_prev = lax.ppermute(key_value, "blk", [(i, i + 1) for i in range(n_blk - 1)])
        from_next = lax.ppermute(key_value, "blk", [(i + 1, i) for i in range(n_blk - 1)])
        window = jnp.concatenate([from_prev, key_value, from_next], axis=1)

        head_count = qkv_weight.shape[2] // HDIM
        query_heads = queries.reshape(tok_rows, head_count, HDIM)
        key_heads = window[0].reshape(3 * tok_rows, head_count, HDIM)
        value_heads = window[1].reshape(3 * tok_rows, head_count, HDIM)
        scores = jnp.einsum(
            "qhd,khd->hqk", query_heads, key_heads, preferred_element_type=jnp.float32
        ) * HDIM ** (-0.5)
        same_request = (query_seg[:, None] == key_seg[None, :])[None, :, :]
        scores = jnp.where(same_request, scores, MASKED)
        maxima = jnp.max(scores, axis=2)
        weights = jnp.where(same_request, jnp.exp(scores - maxima[:, :, None]), 0.0)
        totals = jnp.sum(weights, axis=2)
        mixed = jnp.einsum(
            "hqk,khd->qhd",
            weights.astype(jnp.bfloat16),
            value_heads,
            preferred_element_type=jnp.float32,
        )
        attended = (mixed / jnp.transpose(totals)[:, :, None]).reshape(tok_rows, -1).astype(
            jnp.bfloat16
        )

        chunk_rows = tok_rows // n_tp
        tp_index = lax.axis_index("tp")
        residual = lax.dynamic_slice_in_dim(features, tp_index * chunk_rows, chunk_rows, 0)
        after_attention = residual.astype(jnp.float32) + tp_scatter_sum(
            jnp.dot(attended, out_weight, preferred_element_type=jnp.float32).astype(jnp.bfloat16),
            n_tp,
        )
        normed2 = layer_norm(after_attention, norm2_gain).astype(jnp.bfloat16)
        normed2 = tp_gather_rows(normed2, n_tp).reshape(tok_rows, -1)
        hidden = jax.nn.gelu(
            jnp.dot(normed2, up_weight, preferred_element_type=jnp.float32), approximate=False
        ).astype(jnp.bfloat16)
        after_mlp = after_attention + tp_scatter_sum(
            jnp.dot(hidden, down_weight, preferred_element_type=jnp.float32).astype(jnp.bfloat16),
            n_tp,
        )
        final_norm = layer_norm(after_mlp, merge_gain).astype(jnp.bfloat16)
        final_norm = tp_gather_rows(final_norm, n_tp).reshape(tok_rows, -1)
        group_rows = tok_rows // 4
        grouped = final_norm.reshape(group_rows, 4 * final_norm.shape[1])
        merged = jnp.dot(grouped, merge_weight, preferred_element_type=jnp.float32).astype(
            jnp.bfloat16
        )
        out_width = merged.shape[1]

        all_groups = jnp.arange(n_blk * group_rows, dtype=jnp.int32)
        position = jnp.arange(req_lengths.shape[0], dtype=jnp.int32)
        earlier = (req_owners[None, :] == req_owners[:, None]) & (position[None, :] < position[:, None])
        owner_offset = jnp.sum(jnp.where(earlier, req_lengths[None, :], 0), axis=1)
        shift = req_owners * group_rows + owner_offset - starts
        def target_of(groups):
            inside = (starts[None, :] <= groups[:, None]) & (groups[:, None] < request_ends[None, :])
            return jnp.sum(jnp.where(inside, shift[None, :], 0), axis=1) + groups

        target = target_of(all_groups)

        rounds = group_rows // n_blk
        spread_m = merged.reshape(rounds, n_blk, out_width).transpose(1, 0, 2)
        spread_m = lax.all_to_all(spread_m, "blk", 0, 0, tiled=True)
        spread_m = spread_m.reshape(n_blk * rounds, out_width)
        held_local = jnp.arange(n_blk * rounds, dtype=jnp.int32)
        held_group = (held_local // rounds) * group_rows + (held_local % rounds) * n_blk + my_index
        held_dest = target_of(held_group) // group_rows
        same_dest = held_dest[:, None] == held_dest[None, :]
        before = held_local[None, :] < held_local[:, None]
        held_rank = jnp.sum((same_dest & before).astype(jnp.int32), axis=1)
        capacity = 8
        dest_ids = jnp.arange(n_blk, dtype=jnp.int32)
        cells = jnp.arange(capacity, dtype=jnp.int32)
        hit = (held_dest[None, None, :] == dest_ids[:, None, None]) & (
            held_rank[None, None, :] == cells[None, :, None]
        )
        send_index = jnp.sum(jnp.where(hit, held_local[None, None, :], 0), axis=2)
        send = jnp.take(spread_m, send_index.reshape(-1), axis=0).reshape(n_blk, capacity, out_width)
        received = lax.all_to_all(send, "blk", 0, 0, tiled=True).reshape(n_blk * capacity, out_width)

        my_slots = my_index * group_rows + jnp.arange(group_rows, dtype=jnp.int32)
        source = jnp.sum(
            jnp.where(target[None, :] == my_slots[:, None], all_groups[None, :], 0), axis=1
        )
        source_dev = source % n_blk
        same_src = source_dev[:, None] == source_dev[None, :]
        earlier_src = source[None, :] < source[:, None]
        cell = jnp.sum((same_src & earlier_src).astype(jnp.int32), axis=1)
        return jnp.take(received, source_dev * capacity + cell, axis=0)

    return body


def solution(mesh):
    n_blk = mesh.shape["blk"]
    n_tp = mesh.shape["tp"]
    return jax.shard_map(
        make_body(n_blk, n_tp),
        mesh=mesh,
        in_specs=(
            P("blk", "tp"),
            P(),
            P(),
            P(),
            P(),
            P(None, None, "tp"),
            P("tp", None),
            P(),
            P(None, "tp"),
            P("tp", None),
            P(),
            P(None, "tp"),
        ),
        out_specs=P("blk", "tp"),
        check_vma=False,
    )
```

```python
import jax
import jax.numpy as jnp
from jax import lax
from jax.sharding import PartitionSpec as P

HDIM = 104


EPSILON = 1e-06
MASKED = -1e30
MAX_GROUPS = 125


def layer_norm(values, norm_gain):
    values = values.astype(jnp.float32)
    row_mean = jnp.mean(values, axis=-1, keepdims=True)
    centred = values - row_mean
    spread = jnp.mean(centred * centred, axis=-1, keepdims=True)
    return centred * lax.rsqrt(spread + EPSILON) * norm_gain


def segment_at(positions, request_ends):
    return jnp.sum((request_ends[None, :] <= (positions // 4)[:, None]).astype(jnp.int32), axis=1)


def tp_gather_rows(chunk, n_tp):
    me = lax.axis_index("tp")
    full = jnp.zeros((n_tp,) + chunk.shape, chunk.dtype)
    full = lax.dynamic_update_index_in_dim(full, chunk, me, 0)
    for step in range(1, n_tp):
        got = lax.ppermute(chunk, "tp", [(i, (i + step) % n_tp) for i in range(n_tp)])
        full = lax.dynamic_update_index_in_dim(full, got, (me - step) % n_tp, 0)
    return full


def tp_scatter_sum(partial, n_tp):
    me = lax.axis_index("tp")
    chunks = partial.reshape((n_tp, partial.shape[0] // n_tp) + partial.shape[1:])
    total = lax.dynamic_index_in_dim(chunks, me, 0, keepdims=False).astype(jnp.float32)
    for step in range(1, n_tp):
        send = lax.dynamic_index_in_dim(chunks, (me + step) % n_tp, 0, keepdims=False)
        got = lax.ppermute(send, "tp", [(i, (i + step) % n_tp) for i in range(n_tp)])
        total = total + got.astype(jnp.float32)
    return total


def make_body(n_blk, n_tp):
    def body(
        tokens,
        block_split,
        req_lengths,
        req_owners,
        norm1_gain,
        qkv_weight,
        out_weight,
        norm2_gain,
        up_weight,
        down_weight,
        merge_gain,
        merge_weight,
    ):
        tok_rows, width = tokens.shape
        half_rows = tok_rows // 2
        piece = half_rows // n_blk
        n_slots = block_split.shape[0]
        my_index = lax.axis_index("blk")

        slots = jnp.arange(n_slots, dtype=jnp.int32)
        inverse = jnp.sum(
            jnp.where(block_split[None, :] == slots[:, None], slots[None, :], 0), axis=1
        )
        spread = tokens.reshape(2, n_blk, piece, width).transpose(1, 0, 2, 3)
        spread = lax.all_to_all(spread, "blk", 0, 0, tiled=True)
        spread = spread.reshape(n_slots, piece, width)
        routed = jnp.take(spread, inverse, axis=0).reshape(n_blk, 2, piece, width)
        routed = lax.all_to_all(routed, "blk", 0, 0, tiled=True)
        local = routed.transpose(1, 0, 2, 3).reshape(tok_rows, width)

        request_ends = jnp.cumsum(req_lengths).astype(jnp.int32)
        starts = request_ends - req_lengths
        row_base = my_index * tok_rows
        query_seg = segment_at(row_base + jnp.arange(tok_rows, dtype=jnp.int32), request_ends)
        key_pos = row_base - tok_rows + jnp.arange(3 * tok_rows, dtype=jnp.int32)
        key_valid = (key_pos >= 0) & (key_pos < n_blk * tok_rows)
        key_seg = jnp.where(key_valid, segment_at(key_pos, request_ends), -1)

        stacked = tp_gather_rows(local, n_tp)
        features = stacked.transpose(1, 0, 2).reshape(tok_rows, n_tp * width)
        normed1 = layer_norm(features, norm1_gain).astype(jnp.bfloat16)
        projected = jnp.einsum(
            "td,dcf->ctf", normed1, qkv_weight, preferred_element_type=jnp.float32
        ).astype(jnp.bfloat16)
        queries = projected[0]
        key_value = projected[1:]
        from_prev = lax.ppermute(key_value, "blk", [(i, i + 1) for i in range(n_blk - 1)])
        from_next = lax.ppermute(key_value, "blk", [(i + 1, i) for i in range(n_blk - 1)])
        window = jnp.concatenate([from_prev, key_value, from_next], axis=1)

        head_count = qkv_weight.shape[2] // HDIM
        chunk_rows = tok_rows // n_tp
        key_span = chunk_rows + 2 * (4 * MAX_GROUPS - 1)
        key_span = min(3 * tok_rows, -(-key_span // 128) * 128)
        tp_index = lax.axis_index("tp")

        def attend_chunk(chunk):
            row0 = chunk * chunk_rows
            key0 = jnp.minimum(row0, 3 * tok_rows - key_span)
            query_heads = lax.dynamic_slice_in_dim(queries, row0, chunk_rows, 0).reshape(
                chunk_rows, head_count, HDIM
            )
            seg_q = lax.dynamic_slice_in_dim(query_seg, row0, chunk_rows, 0)
            key_heads = lax.dynamic_slice_in_dim(window[0], key0, key_span, 0).reshape(
                key_span, head_count, HDIM
            )
            value_heads = lax.dynamic_slice_in_dim(window[1], key0, key_span, 0).reshape(
                key_span, head_count, HDIM
            )
            seg_k = lax.dynamic_slice_in_dim(key_seg, key0, key_span, 0)
            scores = jnp.einsum(
                "qhd,khd->hqk", query_heads, key_heads, preferred_element_type=jnp.float32
            ) * HDIM ** (-0.5)
            same_request = (seg_q[:, None] == seg_k[None, :])[None, :, :]
            scores = jnp.where(same_request, scores, MASKED)
            maxima = jnp.max(scores, axis=2)
            weights = jnp.where(same_request, jnp.exp(scores - maxima[:, :, None]), 0.0)
            totals = jnp.sum(weights, axis=2)
            mixed = jnp.einsum(
                "hqk,khd->qhd",
                weights.astype(jnp.bfloat16),
                value_heads,
                preferred_element_type=jnp.float32,
            )
            attended = (mixed / jnp.transpose(totals)[:, :, None]).reshape(chunk_rows, -1)
            return jnp.dot(
                attended.astype(jnp.bfloat16), out_weight, preferred_element_type=jnp.float32
            ).astype(jnp.bfloat16)

        def pairs(step):
            return [(i, (i + step) % n_tp) for i in range(n_tp)]

        far_first = sorted(range(n_tp), key=lambda step: -min(step, n_tp - step))
        attn_sum = None
        for step in far_first:
            part = attend_chunk((tp_index + step) % n_tp)
            if step:
                part = lax.ppermute(part, "tp", pairs(step))
            part = part.astype(jnp.float32)
            attn_sum = part if attn_sum is None else attn_sum + part

        residual = lax.dynamic_slice_in_dim(features, tp_index * chunk_rows, chunk_rows, 0)
        after_attention = residual.astype(jnp.float32) + attn_sum
        normed2 = layer_norm(after_attention, norm2_gain).astype(jnp.bfloat16)
        arrived = {step: lax.ppermute(normed2, "tp", pairs(step)) for step in range(1, n_tp)}
        arrived[0] = normed2
        near_first = sorted(range(n_tp), key=lambda step: min(step, n_tp - step))
        mlp_sum = None
        for step in near_first:
            hidden = jax.nn.gelu(
                jnp.dot(arrived[step], up_weight, preferred_element_type=jnp.float32),
                approximate=False,
            ).astype(jnp.bfloat16)
            part = jnp.dot(hidden, down_weight, preferred_element_type=jnp.float32).astype(
                jnp.bfloat16
            )
            if step:
                part = lax.ppermute(part, "tp", pairs(n_tp - step))
            part = part.astype(jnp.float32)
            mlp_sum = part if mlp_sum is None else mlp_sum + part
        after_mlp = after_attention + mlp_sum
        final_norm = layer_norm(after_mlp, merge_gain).astype(jnp.bfloat16)
        final_norm = tp_gather_rows(final_norm, n_tp).reshape(tok_rows, -1)
        group_rows = tok_rows // 4
        grouped = final_norm.reshape(group_rows, 4 * final_norm.shape[1])
        merged = jnp.dot(grouped, merge_weight, preferred_element_type=jnp.float32).astype(
            jnp.bfloat16
        )
        out_width = merged.shape[1]

        all_groups = jnp.arange(n_blk * group_rows, dtype=jnp.int32)
        position = jnp.arange(req_lengths.shape[0], dtype=jnp.int32)
        earlier = (req_owners[None, :] == req_owners[:, None]) & (position[None, :] < position[:, None])
        owner_offset = jnp.sum(jnp.where(earlier, req_lengths[None, :], 0), axis=1)
        shift = req_owners * group_rows + owner_offset - starts
        def target_of(groups):
            inside = (starts[None, :] <= groups[:, None]) & (groups[:, None] < request_ends[None, :])
            return jnp.sum(jnp.where(inside, shift[None, :], 0), axis=1) + groups

        target = target_of(all_groups)

        rounds = group_rows // n_blk
        spread_m = merged.reshape(rounds, n_blk, out_width).transpose(1, 0, 2)
        spread_m = lax.all_to_all(spread_m, "blk", 0, 0, tiled=True)
        spread_m = spread_m.reshape(n_blk * rounds, out_width)
        held_local = jnp.arange(n_blk * rounds, dtype=jnp.int32)
        held_group = (held_local // rounds) * group_rows + (held_local % rounds) * n_blk + my_index
        held_dest = target_of(held_group) // group_rows
        same_dest = held_dest[:, None] == held_dest[None, :]
        before = held_local[None, :] < held_local[:, None]
        held_rank = jnp.sum((same_dest & before).astype(jnp.int32), axis=1)
        capacity = 8
        dest_ids = jnp.arange(n_blk, dtype=jnp.int32)
        cells = jnp.arange(capacity, dtype=jnp.int32)
        hit = (held_dest[None, None, :] == dest_ids[:, None, None]) & (
            held_rank[None, None, :] == cells[None, :, None]
        )
        send_index = jnp.sum(jnp.where(hit, held_local[None, None, :], 0), axis=2)
        send = jnp.take(spread_m, send_index.reshape(-1), axis=0).reshape(n_blk, capacity, out_width)
        received = lax.all_to_all(send, "blk", 0, 0, tiled=True).reshape(n_blk * capacity, out_width)

        my_slots = my_index * group_rows + jnp.arange(group_rows, dtype=jnp.int32)
        source = jnp.sum(
            jnp.where(target[None, :] == my_slots[:, None], all_groups[None, :], 0), axis=1
        )
        source_dev = source % n_blk
        same_src = source_dev[:, None] == source_dev[None, :]
        earlier_src = source[None, :] < source[:, None]
        cell = jnp.sum((same_src & earlier_src).astype(jnp.int32), axis=1)
        return jnp.take(received, source_dev * capacity + cell, axis=0)

    return body


def solution(mesh):
    n_blk = mesh.shape["blk"]
    n_tp = mesh.shape["tp"]
    return jax.shard_map(
        make_body(n_blk, n_tp),
        mesh=mesh,
        in_specs=(
            P("blk", "tp"),
            P(),
            P(),
            P(),
            P(),
            P(None, None, "tp"),
            P("tp", None),
            P(),
            P(None, "tp"),
            P("tp", None),
            P(),
            P(None, "tp"),
        ),
        out_specs=P("blk", "tp"),
        check_vma=False,
    )
```

```python
import jax
import jax.numpy as jnp
from jax import lax
from jax.sharding import PartitionSpec as P

HDIM = 104


EPSILON = 1e-06
MASKED = -1e30


def layer_norm(values, norm_gain):
    values = values.astype(jnp.float32)
    row_mean = jnp.mean(values, axis=-1, keepdims=True)
    centred = values - row_mean
    spread = jnp.mean(centred * centred, axis=-1, keepdims=True)
    return centred * lax.rsqrt(spread + EPSILON) * norm_gain


def segment_at(positions, request_ends):
    return jnp.sum((request_ends[None, :] <= (positions // 4)[:, None]).astype(jnp.int32), axis=1)


def tp_gather_rows(chunk, n_tp):
    half = chunk.shape[0] // 2
    offloaded = lax.all_gather(chunk[:half], "tp", axis=0, tiled=False)
    return jnp.concatenate([offloaded, tp_permute_rows(chunk[half:], n_tp)], axis=1)


def tp_permute_rows(chunk, n_tp):
    me = lax.axis_index("tp")
    full = jnp.zeros((n_tp,) + chunk.shape, chunk.dtype)
    full = lax.dynamic_update_index_in_dim(full, chunk, me, 0)
    for step in range(1, n_tp):
        got = lax.ppermute(chunk, "tp", [(i, (i + step) % n_tp) for i in range(n_tp)])
        full = lax.dynamic_update_index_in_dim(full, got, (me - step) % n_tp, 0)
    return full


def tp_scatter_sum(partial, n_tp):
    me = lax.axis_index("tp")
    chunks = partial.reshape((n_tp, partial.shape[0] // n_tp) + partial.shape[1:])
    total = lax.dynamic_index_in_dim(chunks, me, 0, keepdims=False).astype(jnp.float32)
    for step in range(1, n_tp):
        send = lax.dynamic_index_in_dim(chunks, (me + step) % n_tp, 0, keepdims=False)
        got = lax.ppermute(send, "tp", [(i, (i + step) % n_tp) for i in range(n_tp)])
        total = total + got.astype(jnp.float32)
    return total


def make_body(n_blk, n_tp):
    def body(
        tokens,
        block_split,
        req_lengths,
        req_owners,
        norm1_gain,
        qkv_weight,
        out_weight,
        norm2_gain,
        up_weight,
        down_weight,
        merge_gain,
        merge_weight,
    ):
        tok_rows, width = tokens.shape
        half_rows = tok_rows // 2
        piece = half_rows // n_blk
        n_slots = block_split.shape[0]
        my_index = lax.axis_index("blk")

        slots = jnp.arange(n_slots, dtype=jnp.int32)
        inverse = jnp.sum(
            jnp.where(block_split[None, :] == slots[:, None], slots[None, :], 0), axis=1
        )
        spread = tokens.reshape(2, n_blk, piece, width).transpose(1, 0, 2, 3)
        spread = lax.all_to_all(spread, "blk", 0, 0, tiled=True)
        spread = spread.reshape(n_slots, piece, width)
        routed = jnp.take(spread, inverse, axis=0).reshape(n_blk, 2, piece, width)
        routed = lax.all_to_all(routed, "blk", 0, 0, tiled=True)
        local = routed.transpose(1, 0, 2, 3).reshape(tok_rows, width)

        request_ends = jnp.cumsum(req_lengths).astype(jnp.int32)
        starts = request_ends - req_lengths
        row_base = my_index * tok_rows
        query_seg = segment_at(row_base + jnp.arange(tok_rows, dtype=jnp.int32), request_ends)
        key_pos = row_base - tok_rows + jnp.arange(3 * tok_rows, dtype=jnp.int32)
        key_valid = (key_pos >= 0) & (key_pos < n_blk * tok_rows)
        key_seg = jnp.where(key_valid, segment_at(key_pos, request_ends), -1)

        stacked = tp_gather_rows(local, n_tp)
        features = stacked.transpose(1, 0, 2).reshape(tok_rows, n_tp * width)
        normed1 = layer_norm(features, norm1_gain).astype(jnp.bfloat16)
        projected = jnp.einsum(
            "td,dcf->ctf", normed1, qkv_weight, preferred_element_type=jnp.float32
        ).astype(jnp.bfloat16)
        queries = projected[0]
        key_value = projected[1:]
        from_prev = lax.ppermute(key_value, "blk", [(i, i + 1) for i in range(n_blk - 1)])
        from_next = lax.ppermute(key_value, "blk", [(i + 1, i) for i in range(n_blk - 1)])
        window = jnp.concatenate([from_prev, key_value, from_next], axis=1)

        head_count = qkv_weight.shape[2] // HDIM
        query_heads = queries.reshape(tok_rows, head_count, HDIM)
        key_heads = window[0].reshape(3 * tok_rows, head_count, HDIM)
        value_heads = window[1].reshape(3 * tok_rows, head_count, HDIM)
        scores = jnp.einsum(
            "qhd,khd->hqk", query_heads, key_heads, preferred_element_type=jnp.float32
        ) * HDIM ** (-0.5)
        same_request = (query_seg[:, None] == key_seg[None, :])[None, :, :]
        scores = jnp.where(same_request, scores, MASKED)
        maxima = jnp.max(scores, axis=2)
        weights = jnp.where(same_request, jnp.exp(scores - maxima[:, :, None]), 0.0)
        totals = jnp.sum(weights, axis=2)
        mixed = jnp.einsum(
            "hqk,khd->qhd",
            weights.astype(jnp.bfloat16),
            value_heads,
            preferred_element_type=jnp.float32,
        )
        attended = (mixed / jnp.transpose(totals)[:, :, None]).reshape(tok_rows, -1).astype(
            jnp.bfloat16
        )

        chunk_rows = tok_rows // n_tp
        tp_index = lax.axis_index("tp")
        residual = lax.dynamic_slice_in_dim(features, tp_index * chunk_rows, chunk_rows, 0)
        after_attention = residual.astype(jnp.float32) + tp_scatter_sum(
            jnp.dot(attended, out_weight, preferred_element_type=jnp.float32).astype(jnp.bfloat16),
            n_tp,
        )
        normed2 = layer_norm(after_attention, norm2_gain).astype(jnp.bfloat16)
        normed2 = tp_gather_rows(normed2, n_tp).reshape(tok_rows, -1)
        hidden = jax.nn.gelu(
            jnp.dot(normed2, up_weight, preferred_element_type=jnp.float32), approximate=False
        ).astype(jnp.bfloat16)
        after_mlp = after_attention + tp_scatter_sum(
            jnp.dot(hidden, down_weight, preferred_element_type=jnp.float32).astype(jnp.bfloat16),
            n_tp,
        )
        final_norm = layer_norm(after_mlp, merge_gain).astype(jnp.bfloat16)
        final_norm = tp_gather_rows(final_norm, n_tp).reshape(tok_rows, -1)
        group_rows = tok_rows // 4
        grouped = final_norm.reshape(group_rows, 4 * final_norm.shape[1])
        merged = jnp.dot(grouped, merge_weight, preferred_element_type=jnp.float32).astype(
            jnp.bfloat16
        )
        out_width = merged.shape[1]

        all_groups = jnp.arange(n_blk * group_rows, dtype=jnp.int32)
        position = jnp.arange(req_lengths.shape[0], dtype=jnp.int32)
        earlier = (req_owners[None, :] == req_owners[:, None]) & (position[None, :] < position[:, None])
        owner_offset = jnp.sum(jnp.where(earlier, req_lengths[None, :], 0), axis=1)
        shift = req_owners * group_rows + owner_offset - starts
        def target_of(groups):
            inside = (starts[None, :] <= groups[:, None]) & (groups[:, None] < request_ends[None, :])
            return jnp.sum(jnp.where(inside, shift[None, :], 0), axis=1) + groups

        target = target_of(all_groups)

        rounds = group_rows // n_blk
        spread_m = merged.reshape(rounds, n_blk, out_width).transpose(1, 0, 2)
        spread_m = lax.all_to_all(spread_m, "blk", 0, 0, tiled=True)
        spread_m = spread_m.reshape(n_blk * rounds, out_width)
        held_local = jnp.arange(n_blk * rounds, dtype=jnp.int32)
        held_group = (held_local // rounds) * group_rows + (held_local % rounds) * n_blk + my_index
        held_dest = target_of(held_group) // group_rows
        same_dest = held_dest[:, None] == held_dest[None, :]
        before = held_local[None, :] < held_local[:, None]
        held_rank = jnp.sum((same_dest & before).astype(jnp.int32), axis=1)
        capacity = 8
        dest_ids = jnp.arange(n_blk, dtype=jnp.int32)
        cells = jnp.arange(capacity, dtype=jnp.int32)
        hit = (held_dest[None, None, :] == dest_ids[:, None, None]) & (
            held_rank[None, None, :] == cells[None, :, None]
        )
        send_index = jnp.sum(jnp.where(hit, held_local[None, None, :], 0), axis=2)
        send = jnp.take(spread_m, send_index.reshape(-1), axis=0).reshape(n_blk, capacity, out_width)
        received = lax.all_to_all(send, "blk", 0, 0, tiled=True).reshape(n_blk * capacity, out_width)

        my_slots = my_index * group_rows + jnp.arange(group_rows, dtype=jnp.int32)
        source = jnp.sum(
            jnp.where(target[None, :] == my_slots[:, None], all_groups[None, :], 0), axis=1
        )
        source_dev = source % n_blk
        same_src = source_dev[:, None] == source_dev[None, :]
        earlier_src = source[None, :] < source[:, None]
        cell = jnp.sum((same_src & earlier_src).astype(jnp.int32), axis=1)
        return jnp.take(received, source_dev * capacity + cell, axis=0)

    return body


def solution(mesh):
    n_blk = mesh.shape["blk"]
    n_tp = mesh.shape["tp"]
    return jax.shard_map(
        make_body(n_blk, n_tp),
        mesh=mesh,
        in_specs=(
            P("blk", "tp"),
            P(),
            P(),
            P(),
            P(),
            P(None, None, "tp"),
            P("tp", None),
            P(),
            P(None, "tp"),
            P("tp", None),
            P(),
            P(None, "tp"),
        ),
        out_specs=P("blk", "tp"),
        check_vma=False,
    )
```

```python
import jax
import jax.numpy as jnp
from jax import lax
from jax.sharding import PartitionSpec as P

HDIM = 104


EPSILON = 1e-06
MASKED = -1e30


def layer_norm(values, norm_gain):
    values = values.astype(jnp.float32)
    row_mean = jnp.mean(values, axis=-1, keepdims=True)
    centred = values - row_mean
    spread = jnp.mean(centred * centred, axis=-1, keepdims=True)
    return centred * lax.rsqrt(spread + EPSILON) * norm_gain


def segment_at(positions, request_ends):
    return jnp.sum((request_ends[None, :] <= (positions // 4)[:, None]).astype(jnp.int32), axis=1)


def tp_gather_rows(chunk, n_tp):
    me = lax.axis_index("tp")
    full = jnp.zeros((n_tp,) + chunk.shape, chunk.dtype)
    full = lax.dynamic_update_index_in_dim(full, chunk, me, 0)
    for step in range(1, n_tp):
        got = lax.ppermute(chunk, "tp", [(i, (i + step) % n_tp) for i in range(n_tp)])
        full = lax.dynamic_update_index_in_dim(full, got, (me - step) % n_tp, 0)
    return full


def tp_scatter_sum(partial, n_tp):
    me = lax.axis_index("tp")
    chunks = partial.reshape((n_tp, partial.shape[0] // n_tp) + partial.shape[1:])
    total = lax.dynamic_index_in_dim(chunks, me, 0, keepdims=False).astype(jnp.float32)
    for step in range(1, n_tp):
        send = lax.dynamic_index_in_dim(chunks, (me + step) % n_tp, 0, keepdims=False)
        got = lax.ppermute(send, "tp", [(i, (i + step) % n_tp) for i in range(n_tp)])
        total = total + got.astype(jnp.float32)
    return total


def tp_gather_rotated(chunk, n_tp):
    blocks = [chunk]
    for step in range(1, n_tp):
        blocks.append(lax.ppermute(chunk, "tp", [(i, (i + step) % n_tp) for i in range(n_tp)]))
    return jnp.concatenate(blocks, axis=0)


def tp_return_sum(partial, n_tp):
    rows = partial.shape[0] // n_tp
    total = partial[:rows].astype(jnp.float32)
    for step in range(1, n_tp):
        got = lax.ppermute(
            partial[step * rows : (step + 1) * rows],
            "tp",
            [(i, (i - step) % n_tp) for i in range(n_tp)],
        )
        total = total + got.astype(jnp.float32)
    return total


def make_body(n_blk, n_tp):
    def body(
        tokens,
        block_split,
        req_lengths,
        req_owners,
        norm1_gain,
        qkv_weight,
        out_weight,
        norm2_gain,
        up_weight,
        down_weight,
        merge_gain,
        merge_weight,
    ):
        tok_rows, width = tokens.shape
        half_rows = tok_rows // 2
        piece = half_rows // n_blk
        n_slots = block_split.shape[0]
        my_index = lax.axis_index("blk")

        slots = jnp.arange(n_slots, dtype=jnp.int32)
        inverse = jnp.sum(
            jnp.where(block_split[None, :] == slots[:, None], slots[None, :], 0), axis=1
        )
        spread = tokens.reshape(2, n_blk, piece, width).transpose(1, 0, 2, 3)
        spread = lax.all_to_all(spread, "blk", 0, 0, tiled=True)
        spread = spread.reshape(n_slots, piece, width)
        routed = jnp.take(spread, inverse, axis=0).reshape(n_blk, 2, piece, width)
        routed = lax.all_to_all(routed, "blk", 0, 0, tiled=True)
        local = routed.transpose(1, 0, 2, 3).reshape(tok_rows, width)

        request_ends = jnp.cumsum(req_lengths).astype(jnp.int32)
        starts = request_ends - req_lengths
        row_base = my_index * tok_rows
        query_seg = segment_at(row_base + jnp.arange(tok_rows, dtype=jnp.int32), request_ends)
        key_pos = row_base - tok_rows + jnp.arange(3 * tok_rows, dtype=jnp.int32)
        key_valid = (key_pos >= 0) & (key_pos < n_blk * tok_rows)
        key_seg = jnp.where(key_valid, segment_at(key_pos, request_ends), -1)

        stacked = tp_gather_rows(local, n_tp)
        features = stacked.transpose(1, 0, 2).reshape(tok_rows, n_tp * width)
        normed1 = layer_norm(features, norm1_gain).astype(jnp.bfloat16)
        projected = jnp.einsum(
            "td,dcf->ctf", normed1, qkv_weight, preferred_element_type=jnp.float32
        ).astype(jnp.bfloat16)
        queries = projected[0]
        key_value = projected[1:]
        from_prev = lax.ppermute(key_value, "blk", [(i, i + 1) for i in range(n_blk - 1)])
        from_next = lax.ppermute(key_value, "blk", [(i + 1, i) for i in range(n_blk - 1)])
        window = jnp.concatenate([from_prev, key_value, from_next], axis=1)

        head_count = qkv_weight.shape[2] // HDIM
        query_heads = queries.reshape(tok_rows, head_count, HDIM)
        key_heads = window[0].reshape(3 * tok_rows, head_count, HDIM)
        value_heads = window[1].reshape(3 * tok_rows, head_count, HDIM)
        scores = jnp.einsum(
            "qhd,khd->hqk", query_heads, key_heads, preferred_element_type=jnp.float32
        ) * HDIM ** (-0.5)
        same_request = (query_seg[:, None] == key_seg[None, :])[None, :, :]
        scores = jnp.where(same_request, scores, MASKED)
        maxima = jnp.max(scores, axis=2)
        weights = jnp.where(same_request, jnp.exp(scores - maxima[:, :, None]), 0.0)
        totals = jnp.sum(weights, axis=2)
        mixed = jnp.einsum(
            "hqk,khd->qhd",
            weights.astype(jnp.bfloat16),
            value_heads,
            preferred_element_type=jnp.float32,
        )
        attended = (mixed / jnp.transpose(totals)[:, :, None]).reshape(tok_rows, -1).astype(
            jnp.bfloat16
        )

        chunk_rows = tok_rows // n_tp
        tp_index = lax.axis_index("tp")
        residual = lax.dynamic_slice_in_dim(features, tp_index * chunk_rows, chunk_rows, 0)
        after_attention = residual.astype(jnp.float32) + tp_scatter_sum(
            jnp.dot(attended, out_weight, preferred_element_type=jnp.float32).astype(jnp.bfloat16),
            n_tp,
        )
        normed2 = layer_norm(after_attention, norm2_gain).astype(jnp.bfloat16)
        normed2 = tp_gather_rotated(normed2, n_tp)
        hidden = jax.nn.gelu(
            jnp.dot(normed2, up_weight, preferred_element_type=jnp.float32), approximate=False
        ).astype(jnp.bfloat16)
        after_mlp = after_attention + tp_return_sum(
            jnp.dot(hidden, down_weight, preferred_element_type=jnp.float32).astype(jnp.bfloat16),
            n_tp,
        )
        final_norm = layer_norm(after_mlp, merge_gain).astype(jnp.bfloat16)
        final_norm = tp_gather_rotated(final_norm, n_tp)
        group_rows = tok_rows // 4
        grouped = final_norm.reshape(group_rows, 4 * final_norm.shape[1])
        merged = jnp.dot(grouped, merge_weight, preferred_element_type=jnp.float32).astype(
            jnp.bfloat16
        )
        out_width = merged.shape[1]
        rotated = merged.reshape(n_tp, group_rows // n_tp, out_width)
        back = (tp_index - jnp.arange(n_tp, dtype=jnp.int32)) % n_tp
        merged = jnp.take(rotated, back, axis=0).reshape(group_rows, out_width)

        all_groups = jnp.arange(n_blk * group_rows, dtype=jnp.int32)
        position = jnp.arange(req_lengths.shape[0], dtype=jnp.int32)
        earlier = (req_owners[None, :] == req_owners[:, None]) & (position[None, :] < position[:, None])
        owner_offset = jnp.sum(jnp.where(earlier, req_lengths[None, :], 0), axis=1)
        shift = req_owners * group_rows + owner_offset - starts
        def target_of(groups):
            inside = (starts[None, :] <= groups[:, None]) & (groups[:, None] < request_ends[None, :])
            return jnp.sum(jnp.where(inside, shift[None, :], 0), axis=1) + groups

        target = target_of(all_groups)

        rounds = group_rows // n_blk
        spread_m = merged.reshape(rounds, n_blk, out_width).transpose(1, 0, 2)
        spread_m = lax.all_to_all(spread_m, "blk", 0, 0, tiled=True)
        spread_m = spread_m.reshape(n_blk * rounds, out_width)
        held_local = jnp.arange(n_blk * rounds, dtype=jnp.int32)
        held_group = (held_local // rounds) * group_rows + (held_local % rounds) * n_blk + my_index
        held_dest = target_of(held_group) // group_rows
        same_dest = held_dest[:, None] == held_dest[None, :]
        before = held_local[None, :] < held_local[:, None]
        held_rank = jnp.sum((same_dest & before).astype(jnp.int32), axis=1)
        capacity = 8
        dest_ids = jnp.arange(n_blk, dtype=jnp.int32)
        cells = jnp.arange(capacity, dtype=jnp.int32)
        hit = (held_dest[None, None, :] == dest_ids[:, None, None]) & (
            held_rank[None, None, :] == cells[None, :, None]
        )
        send_index = jnp.sum(jnp.where(hit, held_local[None, None, :], 0), axis=2)
        send = jnp.take(spread_m, send_index.reshape(-1), axis=0).reshape(n_blk, capacity, out_width)
        received = lax.all_to_all(send, "blk", 0, 0, tiled=True).reshape(n_blk * capacity, out_width)

        my_slots = my_index * group_rows + jnp.arange(group_rows, dtype=jnp.int32)
        source = jnp.sum(
            jnp.where(target[None, :] == my_slots[:, None], all_groups[None, :], 0), axis=1
        )
        source_dev = source % n_blk
        same_src = source_dev[:, None] == source_dev[None, :]
        earlier_src = source[None, :] < source[:, None]
        cell = jnp.sum((same_src & earlier_src).astype(jnp.int32), axis=1)
        return jnp.take(received, source_dev * capacity + cell, axis=0)

    return body


def solution(mesh):
    n_blk = mesh.shape["blk"]
    n_tp = mesh.shape["tp"]
    return jax.shard_map(
        make_body(n_blk, n_tp),
        mesh=mesh,
        in_specs=(
            P("blk", "tp"),
            P(),
            P(),
            P(),
            P(),
            P(None, None, "tp"),
            P("tp", None),
            P(),
            P(None, "tp"),
            P("tp", None),
            P(),
            P(None, "tp"),
        ),
        out_specs=P("blk", "tp"),
        check_vma=False,
    )
```

```python
import jax
import jax.numpy as jnp
from jax import lax
from jax.sharding import PartitionSpec as P

HDIM = 104


EPSILON = 1e-06
MASKED = -1e30


def layer_norm(values, norm_gain):
    values = values.astype(jnp.float32)
    row_mean = jnp.mean(values, axis=-1, keepdims=True)
    centred = values - row_mean
    spread = jnp.mean(centred * centred, axis=-1, keepdims=True)
    return centred * lax.rsqrt(spread + EPSILON) * norm_gain


def segment_at(positions, request_ends):
    return jnp.sum((request_ends[None, :] <= (positions // 4)[:, None]).astype(jnp.int32), axis=1)


def tp_gather_rows(chunk, n_tp):
    me = lax.axis_index("tp")
    full = jnp.zeros((n_tp,) + chunk.shape, chunk.dtype)
    full = lax.dynamic_update_index_in_dim(full, chunk, me, 0)
    for step in range(1, n_tp):
        got = lax.ppermute(chunk, "tp", [(i, (i + step) % n_tp) for i in range(n_tp)])
        full = lax.dynamic_update_index_in_dim(full, got, (me - step) % n_tp, 0)
    return full


def tp_scatter_sum(partial, n_tp):
    me = lax.axis_index("tp")
    chunks = partial.reshape((n_tp, partial.shape[0] // n_tp) + partial.shape[1:])
    total = lax.dynamic_index_in_dim(chunks, me, 0, keepdims=False).astype(jnp.float32)
    for step in range(1, n_tp):
        send = lax.dynamic_index_in_dim(chunks, (me + step) % n_tp, 0, keepdims=False)
        got = lax.ppermute(send, "tp", [(i, (i + step) % n_tp) for i in range(n_tp)])
        total = total + got.astype(jnp.float32)
    return total


def tp_gather_rotated(chunk, n_tp):
    blocks = [chunk]
    for step in range(1, n_tp):
        blocks.append(lax.ppermute(chunk, "tp", [(i, (i + step) % n_tp) for i in range(n_tp)]))
    return jnp.concatenate(blocks, axis=0)


def tp_return_sum(partial, n_tp):
    rows = partial.shape[0] // n_tp
    total = partial[:rows].astype(jnp.float32)
    for step in range(1, n_tp):
        got = lax.ppermute(
            partial[step * rows : (step + 1) * rows],
            "tp",
            [(i, (i - step) % n_tp) for i in range(n_tp)],
        )
        total = total + got.astype(jnp.float32)
    return total


def make_body(n_blk, n_tp):
    def body(
        tokens,
        block_split,
        req_lengths,
        req_owners,
        norm1_gain,
        qkv_weight,
        out_weight,
        norm2_gain,
        up_weight,
        down_weight,
        merge_gain,
        merge_weight,
    ):
        tok_rows, width = tokens.shape
        half_rows = tok_rows // 2
        piece = half_rows // n_blk
        n_slots = block_split.shape[0]
        my_index = lax.axis_index("blk")

        slots = jnp.arange(n_slots, dtype=jnp.int32)
        inverse = jnp.sum(
            jnp.where(block_split[None, :] == slots[:, None], slots[None, :], 0), axis=1
        )
        spread = tokens.reshape(2, n_blk, piece, width).transpose(1, 0, 2, 3)
        spread = lax.all_to_all(spread, "blk", 0, 0, tiled=True)
        spread = spread.reshape(n_slots, piece, width)
        routed = jnp.take(spread, inverse, axis=0).reshape(n_blk, 1, 2, piece, width)
        routed = jnp.broadcast_to(routed, (n_blk, n_tp, 2, piece, width))
        routed = routed.reshape(n_blk * n_tp, 2, piece, width)
        routed = lax.all_to_all(routed, ("blk", "tp"), 0, 0, tiled=True)
        features = (
            routed.reshape(n_blk, n_tp, 2, piece, width)
            .transpose(2, 0, 3, 1, 4)
            .reshape(tok_rows, n_tp * width)
        )

        request_ends = jnp.cumsum(req_lengths).astype(jnp.int32)
        starts = request_ends - req_lengths
        row_base = my_index * tok_rows
        query_seg = segment_at(row_base + jnp.arange(tok_rows, dtype=jnp.int32), request_ends)
        key_pos = row_base - tok_rows + jnp.arange(3 * tok_rows, dtype=jnp.int32)
        key_valid = (key_pos >= 0) & (key_pos < n_blk * tok_rows)
        key_seg = jnp.where(key_valid, segment_at(key_pos, request_ends), -1)

        normed1 = layer_norm(features, norm1_gain).astype(jnp.bfloat16)
        projected = jnp.einsum(
            "td,dcf->ctf", normed1, qkv_weight, preferred_element_type=jnp.float32
        ).astype(jnp.bfloat16)
        queries = projected[0]
        key_value = projected[1:]
        from_prev = lax.ppermute(key_value, "blk", [(i, i + 1) for i in range(n_blk - 1)])
        from_next = lax.ppermute(key_value, "blk", [(i + 1, i) for i in range(n_blk - 1)])
        window = jnp.concatenate([from_prev, key_value, from_next], axis=1)

        head_count = qkv_weight.shape[2] // HDIM
        query_heads = queries.reshape(tok_rows, head_count, HDIM)
        key_heads = window[0].reshape(3 * tok_rows, head_count, HDIM)
        value_heads = window[1].reshape(3 * tok_rows, head_count, HDIM)
        scores = jnp.einsum(
            "qhd,khd->hqk", query_heads, key_heads, preferred_element_type=jnp.float32
        ) * HDIM ** (-0.5)
        same_request = (query_seg[:, None] == key_seg[None, :])[None, :, :]
        scores = jnp.where(same_request, scores, MASKED)
        maxima = jnp.max(scores, axis=2)
        weights = jnp.where(same_request, jnp.exp(scores - maxima[:, :, None]), 0.0)
        totals = jnp.sum(weights, axis=2)
        mixed = jnp.einsum(
            "hqk,khd->qhd",
            weights.astype(jnp.bfloat16),
            value_heads,
            preferred_element_type=jnp.float32,
        )
        attended = (mixed / jnp.transpose(totals)[:, :, None]).reshape(tok_rows, -1).astype(
            jnp.bfloat16
        )

        chunk_rows = tok_rows // n_tp
        tp_index = lax.axis_index("tp")
        residual = lax.dynamic_slice_in_dim(features, tp_index * chunk_rows, chunk_rows, 0)
        after_attention = residual.astype(jnp.float32) + tp_scatter_sum(
            jnp.dot(attended, out_weight, preferred_element_type=jnp.float32).astype(jnp.bfloat16),
            n_tp,
        )
        normed2 = layer_norm(after_attention, norm2_gain).astype(jnp.bfloat16)
        normed2 = tp_gather_rotated(normed2, n_tp)
        hidden = jax.nn.gelu(
            jnp.dot(normed2, up_weight, preferred_element_type=jnp.float32), approximate=False
        ).astype(jnp.bfloat16)
        after_mlp = after_attention + tp_return_sum(
            jnp.dot(hidden, down_weight, preferred_element_type=jnp.float32).astype(jnp.bfloat16),
            n_tp,
        )
        final_norm = layer_norm(after_mlp, merge_gain).astype(jnp.bfloat16)
        final_norm = tp_gather_rotated(final_norm, n_tp)
        group_rows = tok_rows // 4
        grouped = final_norm.reshape(group_rows, 4 * final_norm.shape[1])
        merged = jnp.dot(grouped, merge_weight, preferred_element_type=jnp.float32).astype(
            jnp.bfloat16
        )
        out_width = merged.shape[1]
        rotated = merged.reshape(n_tp, group_rows // n_tp, out_width)
        back = (tp_index - jnp.arange(n_tp, dtype=jnp.int32)) % n_tp
        merged = jnp.take(rotated, back, axis=0).reshape(group_rows, out_width)

        all_groups = jnp.arange(n_blk * group_rows, dtype=jnp.int32)
        position = jnp.arange(req_lengths.shape[0], dtype=jnp.int32)
        earlier = (req_owners[None, :] == req_owners[:, None]) & (position[None, :] < position[:, None])
        owner_offset = jnp.sum(jnp.where(earlier, req_lengths[None, :], 0), axis=1)
        shift = req_owners * group_rows + owner_offset - starts
        def target_of(groups):
            inside = (starts[None, :] <= groups[:, None]) & (groups[:, None] < request_ends[None, :])
            return jnp.sum(jnp.where(inside, shift[None, :], 0), axis=1) + groups

        target = target_of(all_groups)

        rounds = group_rows // n_blk
        spread_m = merged.reshape(rounds, n_blk, out_width).transpose(1, 0, 2)
        spread_m = lax.all_to_all(spread_m, "blk", 0, 0, tiled=True)
        spread_m = spread_m.reshape(n_blk * rounds, out_width)
        held_local = jnp.arange(n_blk * rounds, dtype=jnp.int32)
        held_group = (held_local // rounds) * group_rows + (held_local % rounds) * n_blk + my_index
        held_dest = target_of(held_group) // group_rows
        same_dest = held_dest[:, None] == held_dest[None, :]
        before = held_local[None, :] < held_local[:, None]
        held_rank = jnp.sum((same_dest & before).astype(jnp.int32), axis=1)
        capacity = 8
        dest_ids = jnp.arange(n_blk, dtype=jnp.int32)
        cells = jnp.arange(capacity, dtype=jnp.int32)
        hit = (held_dest[None, None, :] == dest_ids[:, None, None]) & (
            held_rank[None, None, :] == cells[None, :, None]
        )
        send_index = jnp.sum(jnp.where(hit, held_local[None, None, :], 0), axis=2)
        send = jnp.take(spread_m, send_index.reshape(-1), axis=0).reshape(n_blk, capacity, out_width)
        received = lax.all_to_all(send, "blk", 0, 0, tiled=True).reshape(n_blk * capacity, out_width)

        my_slots = my_index * group_rows + jnp.arange(group_rows, dtype=jnp.int32)
        source = jnp.sum(
            jnp.where(target[None, :] == my_slots[:, None], all_groups[None, :], 0), axis=1
        )
        source_dev = source % n_blk
        same_src = source_dev[:, None] == source_dev[None, :]
        earlier_src = source[None, :] < source[:, None]
        cell = jnp.sum((same_src & earlier_src).astype(jnp.int32), axis=1)
        return jnp.take(received, source_dev * capacity + cell, axis=0)

    return body


def solution(mesh):
    n_blk = mesh.shape["blk"]
    n_tp = mesh.shape["tp"]
    return jax.shard_map(
        make_body(n_blk, n_tp),
        mesh=mesh,
        in_specs=(
            P("blk", "tp"),
            P(),
            P(),
            P(),
            P(),
            P(None, None, "tp"),
            P("tp", None),
            P(),
            P(None, "tp"),
            P("tp", None),
            P(),
            P(None, "tp"),
        ),
        out_specs=P("blk", "tp"),
        check_vma=False,
    )
```

```python
import jax
import jax.numpy as jnp
from jax import lax
from jax.sharding import PartitionSpec as P

HDIM = 104


EPSILON = 1e-06
MASKED = -1e30


def layer_norm(values, norm_gain):
    values = values.astype(jnp.float32)
    row_mean = jnp.mean(values, axis=-1, keepdims=True)
    centred = values - row_mean
    spread = jnp.mean(centred * centred, axis=-1, keepdims=True)
    return centred * lax.rsqrt(spread + EPSILON) * norm_gain


def segment_at(positions, request_ends):
    return jnp.sum((request_ends[None, :] <= (positions // 4)[:, None]).astype(jnp.int32), axis=1)


def tp_gather_rows(chunk, n_tp):
    me = lax.axis_index("tp")
    full = jnp.zeros((n_tp,) + chunk.shape, chunk.dtype)
    full = lax.dynamic_update_index_in_dim(full, chunk, me, 0)
    for step in range(1, n_tp):
        got = lax.ppermute(chunk, "tp", [(i, (i + step) % n_tp) for i in range(n_tp)])
        full = lax.dynamic_update_index_in_dim(full, got, (me - step) % n_tp, 0)
    return full


def tp_scatter_sum(partial, n_tp):
    me = lax.axis_index("tp")
    chunks = partial.reshape((n_tp, partial.shape[0] // n_tp) + partial.shape[1:])
    total = lax.dynamic_index_in_dim(chunks, me, 0, keepdims=False).astype(jnp.float32)
    for step in range(1, n_tp):
        send = lax.dynamic_index_in_dim(chunks, (me + step) % n_tp, 0, keepdims=False)
        got = lax.ppermute(send, "tp", [(i, (i + step) % n_tp) for i in range(n_tp)])
        total = total + got.astype(jnp.float32)
    return total


def tp_gather_rotated(chunk, n_tp):
    blocks = [chunk]
    for step in range(1, n_tp):
        blocks.append(lax.ppermute(chunk, "tp", [(i, (i + step) % n_tp) for i in range(n_tp)]))
    return jnp.concatenate(blocks, axis=0)


def tp_return_sum(partial, n_tp):
    rows = partial.shape[0] // n_tp
    total = partial[:rows].astype(jnp.float32)
    for step in range(1, n_tp):
        got = lax.ppermute(
            partial[step * rows : (step + 1) * rows],
            "tp",
            [(i, (i - step) % n_tp) for i in range(n_tp)],
        )
        total = total + got.astype(jnp.float32)
    return total


def make_body(n_blk, n_tp):
    def body(
        tokens,
        block_split,
        req_lengths,
        req_owners,
        norm1_gain,
        qkv_weight,
        out_weight,
        norm2_gain,
        up_weight,
        down_weight,
        merge_gain,
        merge_weight,
    ):
        tok_rows, width = tokens.shape
        half_rows = tok_rows // 2
        piece = half_rows // n_blk
        n_slots = block_split.shape[0]
        my_index = lax.axis_index("blk")

        slots = jnp.arange(n_slots, dtype=jnp.int32)
        inverse = jnp.sum(
            jnp.where(block_split[None, :] == slots[:, None], slots[None, :], 0), axis=1
        )
        spread = tokens.reshape(2, piece, n_blk, width).transpose(2, 0, 1, 3)
        spread = lax.all_to_all(spread, "blk", 0, 0, tiled=True)
        spread = spread.reshape(n_slots, piece, width)
        routed = jnp.take(spread, inverse, axis=0).reshape(n_blk, 2, piece, width)
        routed = jnp.broadcast_to(
            routed.transpose(1, 2, 0, 3)[:, :, :, None, :], (2, piece, n_blk, n_tp, width)
        ).reshape(2, piece, n_blk * n_tp, width)
        routed = lax.all_to_all(routed, ("blk", "tp"), 2, 2, tiled=True)
        features = routed.reshape(tok_rows, n_tp * width)

        request_ends = jnp.cumsum(req_lengths).astype(jnp.int32)
        starts = request_ends - req_lengths
        row_base = my_index * tok_rows
        query_seg = segment_at(row_base + jnp.arange(tok_rows, dtype=jnp.int32), request_ends)
        key_pos = row_base - tok_rows + jnp.arange(3 * tok_rows, dtype=jnp.int32)
        key_valid = (key_pos >= 0) & (key_pos < n_blk * tok_rows)
        key_seg = jnp.where(key_valid, segment_at(key_pos, request_ends), -1)

        normed1 = layer_norm(features, norm1_gain).astype(jnp.bfloat16)
        projected = jnp.einsum(
            "td,dcf->ctf", normed1, qkv_weight, preferred_element_type=jnp.float32
        ).astype(jnp.bfloat16)
        queries = projected[0]
        key_value = projected[1:]
        from_prev = lax.ppermute(key_value, "blk", [(i, i + 1) for i in range(n_blk - 1)])
        from_next = lax.ppermute(key_value, "blk", [(i + 1, i) for i in range(n_blk - 1)])
        window = jnp.concatenate([from_prev, key_value, from_next], axis=1)

        head_count = qkv_weight.shape[2] // HDIM
        query_heads = queries.reshape(tok_rows, head_count, HDIM)
        key_heads = window[0].reshape(3 * tok_rows, head_count, HDIM)
        value_heads = window[1].reshape(3 * tok_rows, head_count, HDIM)
        scores = jnp.einsum(
            "qhd,khd->hqk", query_heads, key_heads, preferred_element_type=jnp.float32
        ) * HDIM ** (-0.5)
        same_request = (query_seg[:, None] == key_seg[None, :])[None, :, :]
        scores = jnp.where(same_request, scores, MASKED)
        maxima = jnp.max(scores, axis=2)
        weights = jnp.where(same_request, jnp.exp(scores - maxima[:, :, None]), 0.0)
        totals = jnp.sum(weights, axis=2)
        mixed = jnp.einsum(
            "hqk,khd->qhd",
            weights.astype(jnp.bfloat16),
            value_heads,
            preferred_element_type=jnp.float32,
        )
        attended = (mixed / jnp.transpose(totals)[:, :, None]).reshape(tok_rows, -1).astype(
            jnp.bfloat16
        )

        chunk_rows = tok_rows // n_tp
        tp_index = lax.axis_index("tp")
        residual = lax.dynamic_slice_in_dim(features, tp_index * chunk_rows, chunk_rows, 0)
        after_attention = residual.astype(jnp.float32) + tp_scatter_sum(
            jnp.dot(attended, out_weight, preferred_element_type=jnp.float32).astype(jnp.bfloat16),
            n_tp,
        )
        normed2 = layer_norm(after_attention, norm2_gain).astype(jnp.bfloat16)
        normed2 = tp_gather_rotated(normed2, n_tp)
        hidden = jax.nn.gelu(
            jnp.dot(normed2, up_weight, preferred_element_type=jnp.float32), approximate=False
        ).astype(jnp.bfloat16)
        after_mlp = after_attention + tp_return_sum(
            jnp.dot(hidden, down_weight, preferred_element_type=jnp.float32).astype(jnp.bfloat16),
            n_tp,
        )
        final_norm = layer_norm(after_mlp, merge_gain).astype(jnp.bfloat16)
        final_norm = tp_gather_rotated(final_norm, n_tp)
        group_rows = tok_rows // 4
        grouped = final_norm.reshape(group_rows, 4 * final_norm.shape[1])
        merged = jnp.dot(grouped, merge_weight, preferred_element_type=jnp.float32).astype(
            jnp.bfloat16
        )
        out_width = merged.shape[1]
        rotated = merged.reshape(n_tp, group_rows // n_tp, out_width)
        back = (tp_index - jnp.arange(n_tp, dtype=jnp.int32)) % n_tp
        merged = jnp.take(rotated, back, axis=0).reshape(group_rows, out_width)

        all_groups = jnp.arange(n_blk * group_rows, dtype=jnp.int32)
        position = jnp.arange(req_lengths.shape[0], dtype=jnp.int32)
        earlier = (req_owners[None, :] == req_owners[:, None]) & (position[None, :] < position[:, None])
        owner_offset = jnp.sum(jnp.where(earlier, req_lengths[None, :], 0), axis=1)
        shift = req_owners * group_rows + owner_offset - starts
        def target_of(groups):
            inside = (starts[None, :] <= groups[:, None]) & (groups[:, None] < request_ends[None, :])
            return jnp.sum(jnp.where(inside, shift[None, :], 0), axis=1) + groups

        target = target_of(all_groups)

        rounds = group_rows // n_blk
        spread_m = merged.reshape(rounds, n_blk, out_width).transpose(1, 0, 2)
        spread_m = lax.all_to_all(spread_m, "blk", 0, 0, tiled=True)
        spread_m = spread_m.reshape(n_blk * rounds, out_width)
        held_local = jnp.arange(n_blk * rounds, dtype=jnp.int32)
        held_group = (held_local // rounds) * group_rows + (held_local % rounds) * n_blk + my_index
        held_dest = target_of(held_group) // group_rows
        same_dest = held_dest[:, None] == held_dest[None, :]
        before = held_local[None, :] < held_local[:, None]
        held_rank = jnp.sum((same_dest & before).astype(jnp.int32), axis=1)
        capacity = 8
        dest_ids = jnp.arange(n_blk, dtype=jnp.int32)
        cells = jnp.arange(capacity, dtype=jnp.int32)
        hit = (held_dest[None, None, :] == dest_ids[:, None, None]) & (
            held_rank[None, None, :] == cells[None, :, None]
        )
        send_index = jnp.sum(jnp.where(hit, held_local[None, None, :], 0), axis=2)
        send = jnp.take(spread_m, send_index.reshape(-1), axis=0).reshape(n_blk, capacity, out_width)
        received = lax.all_to_all(send, "blk", 0, 0, tiled=True).reshape(n_blk * capacity, out_width)

        my_slots = my_index * group_rows + jnp.arange(group_rows, dtype=jnp.int32)
        source = jnp.sum(
            jnp.where(target[None, :] == my_slots[:, None], all_groups[None, :], 0), axis=1
        )
        source_dev = source % n_blk
        same_src = source_dev[:, None] == source_dev[None, :]
        earlier_src = source[None, :] < source[:, None]
        cell = jnp.sum((same_src & earlier_src).astype(jnp.int32), axis=1)
        return jnp.take(received, source_dev * capacity + cell, axis=0)

    return body


def solution(mesh):
    n_blk = mesh.shape["blk"]
    n_tp = mesh.shape["tp"]
    return jax.shard_map(
        make_body(n_blk, n_tp),
        mesh=mesh,
        in_specs=(
            P("blk", "tp"),
            P(),
            P(),
            P(),
            P(),
            P(None, None, "tp"),
            P("tp", None),
            P(),
            P(None, "tp"),
            P("tp", None),
            P(),
            P(None, "tp"),
        ),
        out_specs=P("blk", "tp"),
        check_vma=False,
    )
```

```python
import jax
import jax.numpy as jnp
from jax import lax
from jax.sharding import PartitionSpec as P

HDIM = 104


EPSILON = 1e-06
MASKED = -1e30
MAX_GROUPS = 125


def layer_norm(values, norm_gain):
    values = values.astype(jnp.float32)
    row_mean = jnp.mean(values, axis=-1, keepdims=True)
    centred = values - row_mean
    spread = jnp.mean(centred * centred, axis=-1, keepdims=True)
    return centred * lax.rsqrt(spread + EPSILON) * norm_gain


def segment_at(positions, request_ends):
    return jnp.sum((request_ends[None, :] <= (positions // 4)[:, None]).astype(jnp.int32), axis=1)


def tp_gather_rows(chunk, n_tp):
    me = lax.axis_index("tp")
    full = jnp.zeros((n_tp,) + chunk.shape, chunk.dtype)
    full = lax.dynamic_update_index_in_dim(full, chunk, me, 0)
    for step in range(1, n_tp):
        got = lax.ppermute(chunk, "tp", [(i, (i + step) % n_tp) for i in range(n_tp)])
        full = lax.dynamic_update_index_in_dim(full, got, (me - step) % n_tp, 0)
    return full


def tp_scatter_sum(partial, n_tp):
    me = lax.axis_index("tp")
    chunks = partial.reshape((n_tp, partial.shape[0] // n_tp) + partial.shape[1:])
    total = lax.dynamic_index_in_dim(chunks, me, 0, keepdims=False).astype(jnp.float32)
    for step in range(1, n_tp):
        send = lax.dynamic_index_in_dim(chunks, (me + step) % n_tp, 0, keepdims=False)
        got = lax.ppermute(send, "tp", [(i, (i + step) % n_tp) for i in range(n_tp)])
        total = total + got.astype(jnp.float32)
    return total


def tp_gather_rotated(chunk, n_tp):
    blocks = [chunk]
    for step in range(1, n_tp):
        blocks.append(lax.ppermute(chunk, "tp", [(i, (i + step) % n_tp) for i in range(n_tp)]))
    return jnp.concatenate(blocks, axis=0)


def tp_return_sum(partial, n_tp):
    rows = partial.shape[0] // n_tp
    total = partial[:rows].astype(jnp.float32)
    for step in range(1, n_tp):
        got = lax.ppermute(
            partial[step * rows : (step + 1) * rows],
            "tp",
            [(i, (i - step) % n_tp) for i in range(n_tp)],
        )
        total = total + got.astype(jnp.float32)
    return total


def make_body(n_blk, n_tp):
    def body(
        tokens,
        block_split,
        req_lengths,
        req_owners,
        norm1_gain,
        qkv_weight,
        out_weight,
        norm2_gain,
        up_weight,
        down_weight,
        merge_gain,
        merge_weight,
    ):
        tok_rows, width = tokens.shape
        half_rows = tok_rows // 2
        piece = half_rows // n_blk
        n_slots = block_split.shape[0]
        my_index = lax.axis_index("blk")

        slots = jnp.arange(n_slots, dtype=jnp.int32)
        inverse = jnp.sum(
            jnp.where(block_split[None, :] == slots[:, None], slots[None, :], 0), axis=1
        )
        spread = tokens.reshape(2, n_blk, piece, width).transpose(1, 0, 2, 3)
        spread = lax.all_to_all(spread, "blk", 0, 0, tiled=True)
        spread = spread.reshape(n_slots, piece, width)
        routed = jnp.take(spread, inverse, axis=0).reshape(n_blk, 1, 2, piece, width)
        routed = jnp.broadcast_to(routed, (n_blk, n_tp, 2, piece, width))
        routed = routed.reshape(n_blk * n_tp, 2, piece, width)
        routed = lax.all_to_all(routed, ("blk", "tp"), 0, 0, tiled=True)
        features = (
            routed.reshape(n_blk, n_tp, 2, piece, width)
            .transpose(2, 0, 3, 1, 4)
            .reshape(tok_rows, n_tp * width)
        )

        request_ends = jnp.cumsum(req_lengths).astype(jnp.int32)
        starts = request_ends - req_lengths
        row_base = my_index * tok_rows
        query_seg = segment_at(row_base + jnp.arange(tok_rows, dtype=jnp.int32), request_ends)
        key_pos = row_base - tok_rows + jnp.arange(3 * tok_rows, dtype=jnp.int32)
        key_valid = (key_pos >= 0) & (key_pos < n_blk * tok_rows)
        key_seg = jnp.where(key_valid, segment_at(key_pos, request_ends), -1)

        normed1 = layer_norm(features, norm1_gain).astype(jnp.bfloat16)
        projected = jnp.einsum(
            "td,dcf->ctf", normed1, qkv_weight, preferred_element_type=jnp.float32
        ).astype(jnp.bfloat16)
        queries = projected[0]
        key_value = projected[1:]
        from_prev = lax.ppermute(key_value, "blk", [(i, i + 1) for i in range(n_blk - 1)])
        from_next = lax.ppermute(key_value, "blk", [(i + 1, i) for i in range(n_blk - 1)])
        window = jnp.concatenate([from_prev, key_value, from_next], axis=1)

        head_count = qkv_weight.shape[2] // HDIM
        tp_index = lax.axis_index("tp")
        n_half = 2
        half_rows = tok_rows // n_half
        reach = 4 * MAX_GROUPS - 1
        key_span = min(3 * tok_rows, -(-(half_rows + 2 * reach) // 128) * 128)
        group_rows = tok_rows // 4
        out_width = merge_weight.shape[1]

        def one_half(part):
            row0 = part * half_rows
            key0 = min(row0, 3 * tok_rows - key_span)
            query_heads = queries[row0 : row0 + half_rows].reshape(half_rows, head_count, HDIM)
            seg_q = query_seg[row0 : row0 + half_rows]
            key_heads = window[0, key0 : key0 + key_span].reshape(key_span, head_count, HDIM)
            value_heads = window[1, key0 : key0 + key_span].reshape(key_span, head_count, HDIM)
            seg_k = key_seg[key0 : key0 + key_span]
            scores = jnp.einsum(
                "qhd,khd->hqk", query_heads, key_heads, preferred_element_type=jnp.float32
            ) * HDIM ** (-0.5)
            same_request = (seg_q[:, None] == seg_k[None, :])[None, :, :]
            scores = jnp.where(same_request, scores, MASKED)
            maxima = jnp.max(scores, axis=2)
            weights = jnp.where(same_request, jnp.exp(scores - maxima[:, :, None]), 0.0)
            totals = jnp.sum(weights, axis=2)
            mixed = jnp.einsum(
                "hqk,khd->qhd",
                weights.astype(jnp.bfloat16),
                value_heads,
                preferred_element_type=jnp.float32,
            )
            attended = (mixed / jnp.transpose(totals)[:, :, None]).reshape(half_rows, -1).astype(
                jnp.bfloat16
            )
            chunk_rows = half_rows // n_tp
            residual = lax.dynamic_slice_in_dim(
                features, row0 + tp_index * chunk_rows, chunk_rows, 0
            )
            after_attention = residual.astype(jnp.float32) + tp_scatter_sum(
                jnp.dot(attended, out_weight, preferred_element_type=jnp.float32).astype(
                    jnp.bfloat16
                ),
                n_tp,
            )
            normed2 = layer_norm(after_attention, norm2_gain).astype(jnp.bfloat16)
            normed2 = tp_gather_rotated(normed2, n_tp)
            hidden = jax.nn.gelu(
                jnp.dot(normed2, up_weight, preferred_element_type=jnp.float32), approximate=False
            ).astype(jnp.bfloat16)
            after_mlp = after_attention + tp_return_sum(
                jnp.dot(hidden, down_weight, preferred_element_type=jnp.float32).astype(
                    jnp.bfloat16
                ),
                n_tp,
            )
            final_norm = layer_norm(after_mlp, merge_gain).astype(jnp.bfloat16)
            final_norm = tp_gather_rotated(final_norm, n_tp)
            half_groups = half_rows // 4
            grouped = final_norm.reshape(half_groups, 4 * final_norm.shape[1])
            merged = jnp.dot(grouped, merge_weight, preferred_element_type=jnp.float32).astype(
                jnp.bfloat16
            )
            rotated = merged.reshape(n_tp, half_groups // n_tp, out_width)
            back = (tp_index - jnp.arange(n_tp, dtype=jnp.int32)) % n_tp
            return jnp.take(rotated, back, axis=0).reshape(half_groups, out_width)

        merged = jnp.concatenate([one_half(part) for part in range(n_half)], axis=0)

        all_groups = jnp.arange(n_blk * group_rows, dtype=jnp.int32)
        position = jnp.arange(req_lengths.shape[0], dtype=jnp.int32)
        earlier = (req_owners[None, :] == req_owners[:, None]) & (position[None, :] < position[:, None])
        owner_offset = jnp.sum(jnp.where(earlier, req_lengths[None, :], 0), axis=1)
        shift = req_owners * group_rows + owner_offset - starts
        def target_of(groups):
            inside = (starts[None, :] <= groups[:, None]) & (groups[:, None] < request_ends[None, :])
            return jnp.sum(jnp.where(inside, shift[None, :], 0), axis=1) + groups

        target = target_of(all_groups)

        rounds = group_rows // n_blk
        spread_m = merged.reshape(rounds, n_blk, out_width).transpose(1, 0, 2)
        spread_m = lax.all_to_all(spread_m, "blk", 0, 0, tiled=True)
        spread_m = spread_m.reshape(n_blk * rounds, out_width)
        held_local = jnp.arange(n_blk * rounds, dtype=jnp.int32)
        held_group = (held_local // rounds) * group_rows + (held_local % rounds) * n_blk + my_index
        held_dest = target_of(held_group) // group_rows
        same_dest = held_dest[:, None] == held_dest[None, :]
        before = held_local[None, :] < held_local[:, None]
        held_rank = jnp.sum((same_dest & before).astype(jnp.int32), axis=1)
        capacity = 8
        dest_ids = jnp.arange(n_blk, dtype=jnp.int32)
        cells = jnp.arange(capacity, dtype=jnp.int32)
        hit = (held_dest[None, None, :] == dest_ids[:, None, None]) & (
            held_rank[None, None, :] == cells[None, :, None]
        )
        send_index = jnp.sum(jnp.where(hit, held_local[None, None, :], 0), axis=2)
        send = jnp.take(spread_m, send_index.reshape(-1), axis=0).reshape(n_blk, capacity, out_width)
        received = lax.all_to_all(send, "blk", 0, 0, tiled=True).reshape(n_blk * capacity, out_width)

        my_slots = my_index * group_rows + jnp.arange(group_rows, dtype=jnp.int32)
        source = jnp.sum(
            jnp.where(target[None, :] == my_slots[:, None], all_groups[None, :], 0), axis=1
        )
        source_dev = source % n_blk
        same_src = source_dev[:, None] == source_dev[None, :]
        earlier_src = source[None, :] < source[:, None]
        cell = jnp.sum((same_src & earlier_src).astype(jnp.int32), axis=1)
        return jnp.take(received, source_dev * capacity + cell, axis=0)

    return body


def solution(mesh):
    n_blk = mesh.shape["blk"]
    n_tp = mesh.shape["tp"]
    return jax.shard_map(
        make_body(n_blk, n_tp),
        mesh=mesh,
        in_specs=(
            P("blk", "tp"),
            P(),
            P(),
            P(),
            P(),
            P(None, None, "tp"),
            P("tp", None),
            P(),
            P(None, "tp"),
            P("tp", None),
            P(),
            P(None, "tp"),
        ),
        out_specs=P("blk", "tp"),
        check_vma=False,
    )
```

```python
import jax
import jax.numpy as jnp
from jax import lax
from jax.sharding import PartitionSpec as P

HDIM = 104


EPSILON = 1e-06
MASKED = -1e30
MAX_GROUPS = 125


def layer_norm(values, norm_gain):
    values = values.astype(jnp.float32)
    row_mean = jnp.mean(values, axis=-1, keepdims=True)
    centred = values - row_mean
    spread = jnp.mean(centred * centred, axis=-1, keepdims=True)
    return centred * lax.rsqrt(spread + EPSILON) * norm_gain


def segment_at(positions, request_ends):
    return jnp.sum((request_ends[None, :] <= (positions // 4)[:, None]).astype(jnp.int32), axis=1)


def tp_gather_rows(chunk, n_tp):
    me = lax.axis_index("tp")
    full = jnp.zeros((n_tp,) + chunk.shape, chunk.dtype)
    full = lax.dynamic_update_index_in_dim(full, chunk, me, 0)
    for step in range(1, n_tp):
        got = lax.ppermute(chunk, "tp", [(i, (i + step) % n_tp) for i in range(n_tp)])
        full = lax.dynamic_update_index_in_dim(full, got, (me - step) % n_tp, 0)
    return full


def tp_scatter_sum(partial, n_tp):
    me = lax.axis_index("tp")
    chunks = partial.reshape((n_tp, partial.shape[0] // n_tp) + partial.shape[1:])
    total = lax.dynamic_index_in_dim(chunks, me, 0, keepdims=False).astype(jnp.float32)
    for step in range(1, n_tp):
        send = lax.dynamic_index_in_dim(chunks, (me + step) % n_tp, 0, keepdims=False)
        got = lax.ppermute(send, "tp", [(i, (i + step) % n_tp) for i in range(n_tp)])
        total = total + got.astype(jnp.float32)
    return total


def tp_gather_rotated(chunk, n_tp):
    blocks = [chunk]
    for step in range(1, n_tp):
        blocks.append(lax.ppermute(chunk, "tp", [(i, (i + step) % n_tp) for i in range(n_tp)]))
    return jnp.concatenate(blocks, axis=0)


def tp_return_sum(partial, n_tp):
    rows = partial.shape[0] // n_tp
    total = partial[:rows].astype(jnp.float32)
    for step in range(1, n_tp):
        got = lax.ppermute(
            partial[step * rows : (step + 1) * rows],
            "tp",
            [(i, (i - step) % n_tp) for i in range(n_tp)],
        )
        total = total + got.astype(jnp.float32)
    return total


def make_body(n_blk, n_tp):
    def body(
        tokens,
        block_split,
        req_lengths,
        req_owners,
        norm1_gain,
        qkv_weight,
        out_weight,
        norm2_gain,
        up_weight,
        down_weight,
        merge_gain,
        merge_weight,
    ):
        tok_rows, width = tokens.shape
        half_rows = tok_rows // 2
        piece = half_rows // n_blk
        n_slots = block_split.shape[0]
        my_index = lax.axis_index("blk")

        slots = jnp.arange(n_slots, dtype=jnp.int32)
        inverse = jnp.sum(
            jnp.where(block_split[None, :] == slots[:, None], slots[None, :], 0), axis=1
        )
        spread = tokens.reshape(2, n_blk, piece, width).transpose(1, 0, 2, 3)
        spread = lax.all_to_all(spread, "blk", 0, 0, tiled=True)
        spread = spread.reshape(n_slots, piece, width)
        routed = jnp.take(spread, inverse, axis=0).reshape(n_blk, 1, 2, piece, width)
        routed = jnp.broadcast_to(routed, (n_blk, n_tp, 2, piece, width))
        routed = routed.reshape(n_blk * n_tp, 2, piece, width)
        routed = lax.all_to_all(routed, ("blk", "tp"), 0, 0, tiled=True)
        features = (
            routed.reshape(n_blk, n_tp, 2, piece, width)
            .transpose(2, 0, 3, 1, 4)
            .reshape(tok_rows, n_tp * width)
        )

        request_ends = jnp.cumsum(req_lengths).astype(jnp.int32)
        starts = request_ends - req_lengths
        row_base = my_index * tok_rows
        query_seg = segment_at(row_base + jnp.arange(tok_rows, dtype=jnp.int32), request_ends)
        key_pos = row_base - tok_rows + jnp.arange(3 * tok_rows, dtype=jnp.int32)
        key_valid = (key_pos >= 0) & (key_pos < n_blk * tok_rows)
        key_seg = jnp.where(key_valid, segment_at(key_pos, request_ends), -1)

        normed1 = layer_norm(features, norm1_gain).astype(jnp.bfloat16)
        projected = jnp.einsum(
            "td,dcf->ctf", normed1, qkv_weight, preferred_element_type=jnp.float32
        ).astype(jnp.bfloat16)
        queries = projected[0]
        key_value = projected[1:]
        from_prev = lax.ppermute(key_value, "blk", [(i, i + 1) for i in range(n_blk - 1)])
        from_next = lax.ppermute(key_value, "blk", [(i + 1, i) for i in range(n_blk - 1)])
        window = jnp.concatenate([from_prev, key_value, from_next], axis=1)

        head_count = qkv_weight.shape[2] // HDIM
        tp_index = lax.axis_index("tp")
        n_half = 2
        half_rows = tok_rows // n_half
        reach = 4 * MAX_GROUPS - 1
        key_span = min(3 * tok_rows, -(-(half_rows + 2 * reach) // 128) * 128)
        group_rows = tok_rows // 4
        out_width = merge_weight.shape[1]

        def one_half(part):
            row0 = part * half_rows
            key0 = min(row0, 3 * tok_rows - key_span)
            query_heads = queries[row0 : row0 + half_rows].reshape(half_rows, head_count, HDIM)
            seg_q = query_seg[row0 : row0 + half_rows]
            key_heads = window[0, key0 : key0 + key_span].reshape(key_span, head_count, HDIM)
            value_heads = window[1, key0 : key0 + key_span].reshape(key_span, head_count, HDIM)
            seg_k = key_seg[key0 : key0 + key_span]
            scores = jnp.einsum(
                "qhd,khd->hqk", query_heads, key_heads, preferred_element_type=jnp.float32
            ) * HDIM ** (-0.5)
            same_request = (seg_q[:, None] == seg_k[None, :])[None, :, :]
            scores = jnp.where(same_request, scores, MASKED)
            maxima = jnp.max(scores, axis=2)
            weights = jnp.where(same_request, jnp.exp(scores - maxima[:, :, None]), 0.0)
            totals = jnp.sum(weights, axis=2)
            mixed = jnp.einsum(
                "hqk,khd->qhd",
                weights.astype(jnp.bfloat16),
                value_heads,
                preferred_element_type=jnp.float32,
            )
            attended = (mixed / jnp.transpose(totals)[:, :, None]).reshape(half_rows, -1).astype(
                jnp.bfloat16
            )
            chunk_rows = half_rows // n_tp
            residual = lax.dynamic_slice_in_dim(
                features, row0 + tp_index * chunk_rows, chunk_rows, 0
            )
            after_attention = residual.astype(jnp.float32) + tp_scatter_sum(
                jnp.dot(attended, out_weight, preferred_element_type=jnp.float32).astype(
                    jnp.bfloat16
                ),
                n_tp,
            )
            normed2 = layer_norm(after_attention, norm2_gain).astype(jnp.bfloat16)
            normed2 = tp_gather_rotated(normed2, n_tp)
            hidden = jax.nn.gelu(
                jnp.dot(normed2, up_weight, preferred_element_type=jnp.float32), approximate=False
            ).astype(jnp.bfloat16)
            after_mlp = after_attention + tp_return_sum(
                jnp.dot(hidden, down_weight, preferred_element_type=jnp.float32).astype(
                    jnp.bfloat16
                ),
                n_tp,
            )
            final_norm = layer_norm(after_mlp, merge_gain).astype(jnp.bfloat16)
            return tp_gather_rotated(final_norm, n_tp)

        final_norm = jnp.concatenate([one_half(part) for part in range(n_half)], axis=0)
        grouped = final_norm.reshape(group_rows, 4 * final_norm.shape[1])
        merged = jnp.dot(grouped, merge_weight, preferred_element_type=jnp.float32).astype(
            jnp.bfloat16
        )
        rotated = merged.reshape(n_half, n_tp, group_rows // (n_half * n_tp), out_width)
        back = (tp_index - jnp.arange(n_tp, dtype=jnp.int32)) % n_tp
        merged = jnp.take(rotated, back, axis=1).reshape(group_rows, out_width)

        all_groups = jnp.arange(n_blk * group_rows, dtype=jnp.int32)
        position = jnp.arange(req_lengths.shape[0], dtype=jnp.int32)
        earlier = (req_owners[None, :] == req_owners[:, None]) & (position[None, :] < position[:, None])
        owner_offset = jnp.sum(jnp.where(earlier, req_lengths[None, :], 0), axis=1)
        shift = req_owners * group_rows + owner_offset - starts
        def target_of(groups):
            inside = (starts[None, :] <= groups[:, None]) & (groups[:, None] < request_ends[None, :])
            return jnp.sum(jnp.where(inside, shift[None, :], 0), axis=1) + groups

        target = target_of(all_groups)

        rounds = group_rows // n_blk
        spread_m = merged.reshape(rounds, n_blk, out_width).transpose(1, 0, 2)
        spread_m = lax.all_to_all(spread_m, "blk", 0, 0, tiled=True)
        spread_m = spread_m.reshape(n_blk * rounds, out_width)
        held_local = jnp.arange(n_blk * rounds, dtype=jnp.int32)
        held_group = (held_local // rounds) * group_rows + (held_local % rounds) * n_blk + my_index
        held_dest = target_of(held_group) // group_rows
        same_dest = held_dest[:, None] == held_dest[None, :]
        before = held_local[None, :] < held_local[:, None]
        held_rank = jnp.sum((same_dest & before).astype(jnp.int32), axis=1)
        capacity = 8
        dest_ids = jnp.arange(n_blk, dtype=jnp.int32)
        cells = jnp.arange(capacity, dtype=jnp.int32)
        hit = (held_dest[None, None, :] == dest_ids[:, None, None]) & (
            held_rank[None, None, :] == cells[None, :, None]
        )
        send_index = jnp.sum(jnp.where(hit, held_local[None, None, :], 0), axis=2)
        send = jnp.take(spread_m, send_index.reshape(-1), axis=0).reshape(n_blk, capacity, out_width)
        received = lax.all_to_all(send, "blk", 0, 0, tiled=True).reshape(n_blk * capacity, out_width)

        my_slots = my_index * group_rows + jnp.arange(group_rows, dtype=jnp.int32)
        source = jnp.sum(
            jnp.where(target[None, :] == my_slots[:, None], all_groups[None, :], 0), axis=1
        )
        source_dev = source % n_blk
        same_src = source_dev[:, None] == source_dev[None, :]
        earlier_src = source[None, :] < source[:, None]
        cell = jnp.sum((same_src & earlier_src).astype(jnp.int32), axis=1)
        return jnp.take(received, source_dev * capacity + cell, axis=0)

    return body


def solution(mesh):
    n_blk = mesh.shape["blk"]
    n_tp = mesh.shape["tp"]
    return jax.shard_map(
        make_body(n_blk, n_tp),
        mesh=mesh,
        in_specs=(
            P("blk", "tp"),
            P(),
            P(),
            P(),
            P(),
            P(None, None, "tp"),
            P("tp", None),
            P(),
            P(None, "tp"),
            P("tp", None),
            P(),
            P(None, "tp"),
        ),
        out_specs=P("blk", "tp"),
        check_vma=False,
    )
```

```python
import jax
import jax.numpy as jnp
from jax import lax
from jax.sharding import PartitionSpec as P

HDIM = 104


EPSILON = 1e-06
MASKED = -1e30
MAX_GROUPS = 125


def layer_norm(values, norm_gain):
    values = values.astype(jnp.float32)
    row_mean = jnp.mean(values, axis=-1, keepdims=True)
    centred = values - row_mean
    spread = jnp.mean(centred * centred, axis=-1, keepdims=True)
    return centred * lax.rsqrt(spread + EPSILON) * norm_gain


def segment_at(positions, request_ends):
    return jnp.sum((request_ends[None, :] <= (positions // 4)[:, None]).astype(jnp.int32), axis=1)


def tp_gather_rows(chunk, n_tp):
    me = lax.axis_index("tp")
    full = jnp.zeros((n_tp,) + chunk.shape, chunk.dtype)
    full = lax.dynamic_update_index_in_dim(full, chunk, me, 0)
    for step in range(1, n_tp):
        got = lax.ppermute(chunk, "tp", [(i, (i + step) % n_tp) for i in range(n_tp)])
        full = lax.dynamic_update_index_in_dim(full, got, (me - step) % n_tp, 0)
    return full


def tp_scatter_sum(partial, n_tp):
    me = lax.axis_index("tp")
    chunks = partial.reshape((n_tp, partial.shape[0] // n_tp) + partial.shape[1:])
    total = lax.dynamic_index_in_dim(chunks, me, 0, keepdims=False).astype(jnp.float32)
    for step in range(1, n_tp):
        send = lax.dynamic_index_in_dim(chunks, (me + step) % n_tp, 0, keepdims=False)
        got = lax.ppermute(send, "tp", [(i, (i + step) % n_tp) for i in range(n_tp)])
        total = total + got.astype(jnp.float32)
    return total


def tp_gather_rotated(chunk, n_tp):
    blocks = [chunk]
    for step in range(1, n_tp):
        blocks.append(lax.ppermute(chunk, "tp", [(i, (i + step) % n_tp) for i in range(n_tp)]))
    return jnp.concatenate(blocks, axis=0)


def tp_return_sum(partial, n_tp):
    rows = partial.shape[0] // n_tp
    total = partial[:rows].astype(jnp.float32)
    for step in range(1, n_tp):
        got = lax.ppermute(
            partial[step * rows : (step + 1) * rows],
            "tp",
            [(i, (i - step) % n_tp) for i in range(n_tp)],
        )
        total = total + got.astype(jnp.float32)
    return total


def make_body(n_blk, n_tp):
    def body(
        tokens,
        block_split,
        req_lengths,
        req_owners,
        norm1_gain,
        qkv_weight,
        out_weight,
        norm2_gain,
        up_weight,
        down_weight,
        merge_gain,
        merge_weight,
    ):
        tok_rows, width = tokens.shape
        half_rows = tok_rows // 2
        piece = half_rows // n_blk
        n_slots = block_split.shape[0]
        my_index = lax.axis_index("blk")

        slots = jnp.arange(n_slots, dtype=jnp.int32)
        inverse = jnp.sum(
            jnp.where(block_split[None, :] == slots[:, None], slots[None, :], 0), axis=1
        )
        spread = tokens.reshape(2, n_blk, piece, width).transpose(1, 0, 2, 3)
        spread = lax.all_to_all(spread, "blk", 0, 0, tiled=True)
        spread = spread.reshape(n_slots, piece, width)
        routed = jnp.take(spread, inverse, axis=0).reshape(n_blk, 1, 2, piece, width)
        routed = jnp.broadcast_to(routed, (n_blk, n_tp, 2, piece, width))
        routed = routed.reshape(n_blk * n_tp, 2, piece, width)
        routed = lax.all_to_all(routed, ("blk", "tp"), 0, 0, tiled=True)
        features = (
            routed.reshape(n_blk, n_tp, 2, piece, width)
            .transpose(2, 0, 3, 1, 4)
            .reshape(tok_rows, n_tp * width)
        )

        request_ends = jnp.cumsum(req_lengths).astype(jnp.int32)
        starts = request_ends - req_lengths
        row_base = my_index * tok_rows
        query_seg = segment_at(row_base + jnp.arange(tok_rows, dtype=jnp.int32), request_ends)
        key_pos = row_base - tok_rows + jnp.arange(3 * tok_rows, dtype=jnp.int32)
        key_valid = (key_pos >= 0) & (key_pos < n_blk * tok_rows)
        key_seg = jnp.where(key_valid, segment_at(key_pos, request_ends), -1)

        normed1 = layer_norm(features, norm1_gain).astype(jnp.bfloat16)
        key_value = jnp.einsum(
            "td,dcf->ctf", normed1, qkv_weight[:, 1:], preferred_element_type=jnp.float32
        ).astype(jnp.bfloat16)
        queries = jnp.dot(normed1, qkv_weight[:, 0], preferred_element_type=jnp.float32).astype(
            jnp.bfloat16
        )
        from_prev = lax.ppermute(key_value, "blk", [(i, i + 1) for i in range(n_blk - 1)])
        from_next = lax.ppermute(key_value, "blk", [(i + 1, i) for i in range(n_blk - 1)])
        window = jnp.concatenate([from_prev, key_value, from_next], axis=1)

        head_count = qkv_weight.shape[2] // HDIM
        tp_index = lax.axis_index("tp")
        n_half = 2
        half_rows = tok_rows // n_half
        reach = 4 * MAX_GROUPS - 1
        key_span = min(3 * tok_rows, -(-(half_rows + 2 * reach) // 128) * 128)
        group_rows = tok_rows // 4
        out_width = merge_weight.shape[1]

        def one_half(part):
            row0 = part * half_rows
            key0 = min(row0, 3 * tok_rows - key_span)
            query_heads = queries[row0 : row0 + half_rows].reshape(half_rows, head_count, HDIM)
            seg_q = query_seg[row0 : row0 + half_rows]
            key_heads = window[0, key0 : key0 + key_span].reshape(key_span, head_count, HDIM)
            value_heads = window[1, key0 : key0 + key_span].reshape(key_span, head_count, HDIM)
            seg_k = key_seg[key0 : key0 + key_span]
            scores = jnp.einsum(
                "qhd,khd->hqk", query_heads, key_heads, preferred_element_type=jnp.float32
            ) * HDIM ** (-0.5)
            same_request = (seg_q[:, None] == seg_k[None, :])[None, :, :]
            scores = jnp.where(same_request, scores, MASKED)
            maxima = jnp.max(scores, axis=2)
            weights = jnp.where(same_request, jnp.exp(scores - maxima[:, :, None]), 0.0)
            totals = jnp.sum(weights, axis=2)
            mixed = jnp.einsum(
                "hqk,khd->qhd",
                weights.astype(jnp.bfloat16),
                value_heads,
                preferred_element_type=jnp.float32,
            )
            attended = (mixed / jnp.transpose(totals)[:, :, None]).reshape(half_rows, -1).astype(
                jnp.bfloat16
            )
            chunk_rows = half_rows // n_tp
            residual = lax.dynamic_slice_in_dim(
                features, row0 + tp_index * chunk_rows, chunk_rows, 0
            )
            after_attention = residual.astype(jnp.float32) + tp_scatter_sum(
                jnp.dot(attended, out_weight, preferred_element_type=jnp.float32).astype(
                    jnp.bfloat16
                ),
                n_tp,
            )
            normed2 = layer_norm(after_attention, norm2_gain).astype(jnp.bfloat16)
            normed2 = tp_gather_rotated(normed2, n_tp)
            hidden = jax.nn.gelu(
                jnp.dot(normed2, up_weight, preferred_element_type=jnp.float32), approximate=False
            ).astype(jnp.bfloat16)
            after_mlp = after_attention + tp_return_sum(
                jnp.dot(hidden, down_weight, preferred_element_type=jnp.float32).astype(
                    jnp.bfloat16
                ),
                n_tp,
            )
            final_norm = layer_norm(after_mlp, merge_gain).astype(jnp.bfloat16)
            final_norm = tp_gather_rotated(final_norm, n_tp)
            half_groups = half_rows // 4
            grouped = final_norm.reshape(half_groups, 4 * final_norm.shape[1])
            merged = jnp.dot(grouped, merge_weight, preferred_element_type=jnp.float32).astype(
                jnp.bfloat16
            )
            rotated = merged.reshape(n_tp, half_groups // n_tp, out_width)
            back = (tp_index - jnp.arange(n_tp, dtype=jnp.int32)) % n_tp
            return jnp.take(rotated, back, axis=0).reshape(half_groups, out_width)

        merged = jnp.concatenate([one_half(part) for part in range(n_half)], axis=0)

        all_groups = jnp.arange(n_blk * group_rows, dtype=jnp.int32)
        position = jnp.arange(req_lengths.shape[0], dtype=jnp.int32)
        earlier = (req_owners[None, :] == req_owners[:, None]) & (position[None, :] < position[:, None])
        owner_offset = jnp.sum(jnp.where(earlier, req_lengths[None, :], 0), axis=1)
        shift = req_owners * group_rows + owner_offset - starts
        def target_of(groups):
            inside = (starts[None, :] <= groups[:, None]) & (groups[:, None] < request_ends[None, :])
            return jnp.sum(jnp.where(inside, shift[None, :], 0), axis=1) + groups

        target = target_of(all_groups)

        rounds = group_rows // n_blk
        spread_m = merged.reshape(rounds, n_blk, out_width).transpose(1, 0, 2)
        spread_m = lax.all_to_all(spread_m, "blk", 0, 0, tiled=True)
        spread_m = spread_m.reshape(n_blk * rounds, out_width)
        held_local = jnp.arange(n_blk * rounds, dtype=jnp.int32)
        held_group = (held_local // rounds) * group_rows + (held_local % rounds) * n_blk + my_index
        held_dest = target_of(held_group) // group_rows
        same_dest = held_dest[:, None] == held_dest[None, :]
        before = held_local[None, :] < held_local[:, None]
        held_rank = jnp.sum((same_dest & before).astype(jnp.int32), axis=1)
        capacity = 7
        dest_ids = jnp.arange(n_blk, dtype=jnp.int32)
        cells = jnp.arange(capacity, dtype=jnp.int32)
        hit = (held_dest[None, None, :] == dest_ids[:, None, None]) & (
            held_rank[None, None, :] == cells[None, :, None]
        )
        send_index = jnp.sum(jnp.where(hit, held_local[None, None, :], 0), axis=2)
        send = jnp.take(spread_m, send_index.reshape(-1), axis=0).reshape(n_blk, capacity, out_width)
        received = lax.all_to_all(send, "blk", 0, 0, tiled=True).reshape(n_blk * capacity, out_width)

        my_slots = my_index * group_rows + jnp.arange(group_rows, dtype=jnp.int32)
        source = jnp.sum(
            jnp.where(target[None, :] == my_slots[:, None], all_groups[None, :], 0), axis=1
        )
        source_dev = source % n_blk
        same_src = source_dev[:, None] == source_dev[None, :]
        earlier_src = source[None, :] < source[:, None]
        cell = jnp.sum((same_src & earlier_src).astype(jnp.int32), axis=1)
        return jnp.take(received, source_dev * capacity + cell, axis=0)

    return body


def solution(mesh):
    n_blk = mesh.shape["blk"]
    n_tp = mesh.shape["tp"]
    return jax.shard_map(
        make_body(n_blk, n_tp),
        mesh=mesh,
        in_specs=(
            P("blk", "tp"),
            P(),
            P(),
            P(),
            P(),
            P(None, None, "tp"),
            P("tp", None),
            P(),
            P(None, "tp"),
            P("tp", None),
            P(),
            P(None, "tp"),
        ),
        out_specs=P("blk", "tp"),
        check_vma=False,
    )
```

```python
import jax
import jax.numpy as jnp
from jax import lax
from jax.sharding import PartitionSpec as P

HDIM = 104


EPSILON = 1e-06
MASKED = -1e30
MAX_GROUPS = 125


def layer_norm(values, norm_gain):
    values = values.astype(jnp.float32)
    row_mean = jnp.mean(values, axis=-1, keepdims=True)
    centred = values - row_mean
    spread = jnp.mean(centred * centred, axis=-1, keepdims=True)
    return centred * lax.rsqrt(spread + EPSILON) * norm_gain


def segment_at(positions, request_ends):
    return jnp.sum((request_ends[None, :] <= (positions // 4)[:, None]).astype(jnp.int32), axis=1)


def tp_gather_rows(chunk, n_tp):
    me = lax.axis_index("tp")
    full = jnp.zeros((n_tp,) + chunk.shape, chunk.dtype)
    full = lax.dynamic_update_index_in_dim(full, chunk, me, 0)
    for step in range(1, n_tp):
        got = lax.ppermute(chunk, "tp", [(i, (i + step) % n_tp) for i in range(n_tp)])
        full = lax.dynamic_update_index_in_dim(full, got, (me - step) % n_tp, 0)
    return full


def tp_scatter_sum(partial, n_tp):
    me = lax.axis_index("tp")
    chunks = partial.reshape((n_tp, partial.shape[0] // n_tp) + partial.shape[1:])
    total = lax.dynamic_index_in_dim(chunks, me, 0, keepdims=False).astype(jnp.float32)
    for step in range(1, n_tp):
        send = lax.dynamic_index_in_dim(chunks, (me + step) % n_tp, 0, keepdims=False)
        got = lax.ppermute(send, "tp", [(i, (i + step) % n_tp) for i in range(n_tp)])
        total = total + got.astype(jnp.float32)
    return total


def tp_gather_rotated(chunk, n_tp):
    blocks = [chunk]
    for step in range(1, n_tp):
        blocks.append(lax.ppermute(chunk, "tp", [(i, (i + step) % n_tp) for i in range(n_tp)]))
    return jnp.concatenate(blocks, axis=0)


def tp_return_sum(partial, n_tp):
    rows = partial.shape[0] // n_tp
    total = partial[:rows].astype(jnp.float32)
    for step in range(1, n_tp):
        got = lax.ppermute(
            partial[step * rows : (step + 1) * rows],
            "tp",
            [(i, (i - step) % n_tp) for i in range(n_tp)],
        )
        total = total + got.astype(jnp.float32)
    return total


def make_body(n_blk, n_tp):
    def body(
        tokens,
        block_split,
        req_lengths,
        req_owners,
        norm1_gain,
        qkv_weight,
        out_weight,
        norm2_gain,
        up_weight,
        down_weight,
        merge_gain,
        merge_weight,
    ):
        tok_rows, width = tokens.shape
        half_rows = tok_rows // 2
        piece = half_rows // n_blk
        n_slots = block_split.shape[0]
        my_index = lax.axis_index("blk")

        slots = jnp.arange(n_slots, dtype=jnp.int32)
        inverse = jnp.sum(
            jnp.where(block_split[None, :] == slots[:, None], slots[None, :], 0), axis=1
        )
        spread = tokens.reshape(2, n_blk, piece, width).transpose(1, 0, 2, 3)
        spread = lax.all_to_all(spread, "blk", 0, 0, tiled=True)
        spread = spread.reshape(n_slots, piece, width)
        routed = jnp.take(spread, inverse, axis=0).reshape(n_blk, 1, 2, piece, width)
        routed = jnp.broadcast_to(routed, (n_blk, n_tp, 2, piece, width))
        routed = routed.reshape(n_blk * n_tp, 2, piece, width)
        routed = lax.all_to_all(routed, ("blk", "tp"), 0, 0, tiled=True)
        features = (
            routed.reshape(n_blk, n_tp, 2, piece, width)
            .transpose(2, 0, 3, 1, 4)
            .reshape(tok_rows, n_tp * width)
        )

        request_ends = jnp.cumsum(req_lengths).astype(jnp.int32)
        starts = request_ends - req_lengths
        row_base = my_index * tok_rows
        query_seg = segment_at(row_base + jnp.arange(tok_rows, dtype=jnp.int32), request_ends)
        key_pos = row_base - tok_rows + jnp.arange(3 * tok_rows, dtype=jnp.int32)
        key_valid = (key_pos >= 0) & (key_pos < n_blk * tok_rows)
        key_seg = jnp.where(key_valid, segment_at(key_pos, request_ends), -1)

        normed1 = layer_norm(features, norm1_gain).astype(jnp.bfloat16)
        projected = jnp.einsum(
            "td,dcf->ctf", normed1, qkv_weight, preferred_element_type=jnp.float32
        ).astype(jnp.bfloat16)
        queries = projected[0]
        key_value = projected[1:]
        from_prev = lax.ppermute(key_value, "blk", [(i, i + 1) for i in range(n_blk - 1)])
        from_next = lax.ppermute(key_value, "blk", [(i + 1, i) for i in range(n_blk - 1)])
        window = jnp.concatenate([from_prev, key_value, from_next], axis=1)

        head_count = qkv_weight.shape[2] // HDIM
        tp_index = lax.axis_index("tp")
        n_half = 2
        half_rows = tok_rows // n_half
        reach = 4 * MAX_GROUPS - 1
        key_span = min(3 * tok_rows, -(-(half_rows + 2 * reach) // 128) * 128)
        group_rows = tok_rows // 4
        out_width = merge_weight.shape[1]

        def one_half(part):
            row0 = part * half_rows
            key0 = min(row0, 3 * tok_rows - key_span)
            query_heads = queries[row0 : row0 + half_rows].reshape(half_rows, head_count, HDIM)
            seg_q = query_seg[row0 : row0 + half_rows]
            key_heads = window[0, key0 : key0 + key_span].reshape(key_span, head_count, HDIM)
            value_heads = window[1, key0 : key0 + key_span].reshape(key_span, head_count, HDIM)
            seg_k = key_seg[key0 : key0 + key_span]
            scores = jnp.einsum(
                "qhd,khd->hqk", query_heads, key_heads, preferred_element_type=jnp.float32
            ) * HDIM ** (-0.5)
            same_request = (seg_q[:, None] == seg_k[None, :])[None, :, :]
            scores = jnp.where(same_request, scores, MASKED)
            maxima = jnp.max(scores, axis=2)
            weights = jnp.where(same_request, jnp.exp(scores - maxima[:, :, None]), 0.0)
            totals = jnp.sum(weights, axis=2)
            mixed = jnp.einsum(
                "hqk,khd->qhd",
                weights.astype(jnp.bfloat16),
                value_heads,
                preferred_element_type=jnp.float32,
            )
            attended = (mixed / jnp.transpose(totals)[:, :, None]).reshape(half_rows, -1).astype(
                jnp.bfloat16
            )
            chunk_rows = half_rows // n_tp
            residual = lax.dynamic_slice_in_dim(
                features, row0 + tp_index * chunk_rows, chunk_rows, 0
            )
            after_attention = residual.astype(jnp.float32) + tp_scatter_sum(
                jnp.dot(attended, out_weight, preferred_element_type=jnp.float32).astype(
                    jnp.bfloat16
                ),
                n_tp,
            )
            normed2 = layer_norm(after_attention, norm2_gain).astype(jnp.bfloat16)
            normed2 = tp_gather_rotated(normed2, n_tp)
            hidden = jax.nn.gelu(
                jnp.dot(normed2, up_weight, preferred_element_type=jnp.float32), approximate=False
            ).astype(jnp.bfloat16)
            after_mlp = after_attention + tp_return_sum(
                jnp.dot(hidden, down_weight, preferred_element_type=jnp.float32).astype(
                    jnp.bfloat16
                ),
                n_tp,
            )
            final_norm = layer_norm(after_mlp, merge_gain).astype(jnp.bfloat16)
            final_norm = tp_gather_rotated(final_norm, n_tp)
            half_groups = half_rows // 4
            grouped = final_norm.reshape(half_groups, 4 * final_norm.shape[1])
            merged = jnp.dot(grouped, merge_weight, preferred_element_type=jnp.float32).astype(
                jnp.bfloat16
            )
            rotated = merged.reshape(n_tp, half_groups // n_tp, out_width)
            back = (tp_index - jnp.arange(n_tp, dtype=jnp.int32)) % n_tp
            return jnp.take(rotated, back, axis=0).reshape(half_groups, out_width)

        merged = jnp.concatenate([one_half(part) for part in range(n_half)], axis=0)

        all_groups = jnp.arange(n_blk * group_rows, dtype=jnp.int32)
        position = jnp.arange(req_lengths.shape[0], dtype=jnp.int32)
        earlier = (req_owners[None, :] == req_owners[:, None]) & (position[None, :] < position[:, None])
        owner_offset = jnp.sum(jnp.where(earlier, req_lengths[None, :], 0), axis=1)
        shift = req_owners * group_rows + owner_offset - starts
        def target_of(groups):
            inside = (starts[None, :] <= groups[:, None]) & (groups[:, None] < request_ends[None, :])
            return jnp.sum(jnp.where(inside, shift[None, :], 0), axis=1) + groups

        target = target_of(all_groups)

        rounds = group_rows // n_blk
        spread_m = merged.reshape(rounds, n_blk, out_width).transpose(1, 0, 2)
        spread_m = lax.all_to_all(spread_m, "blk", 0, 0, tiled=True)
        spread_m = spread_m.reshape(n_blk * rounds, out_width)
        held_local = jnp.arange(n_blk * rounds, dtype=jnp.int32)
        held_group = (held_local // rounds) * group_rows + (held_local % rounds) * n_blk + my_index
        held_dest = target_of(held_group) // group_rows
        same_dest = held_dest[:, None] == held_dest[None, :]
        before = held_local[None, :] < held_local[:, None]
        held_rank = jnp.sum((same_dest & before).astype(jnp.int32), axis=1)
        capacity = 7
        dest_ids = jnp.arange(n_blk, dtype=jnp.int32)
        cells = jnp.arange(capacity, dtype=jnp.int32)
        hit = (held_dest[None, None, :] == dest_ids[:, None, None]) & (
            held_rank[None, None, :] == cells[None, :, None]
        )
        send_index = jnp.sum(jnp.where(hit, held_local[None, None, :], 0), axis=2)
        send = jnp.take(spread_m, send_index.reshape(-1), axis=0).reshape(n_blk, capacity, out_width)
        received = lax.all_to_all(send, "blk", 0, 0, tiled=True).reshape(n_blk * capacity, out_width)

        my_slots = my_index * group_rows + jnp.arange(group_rows, dtype=jnp.int32)
        source = jnp.sum(
            jnp.where(target[None, :] == my_slots[:, None], all_groups[None, :], 0), axis=1
        )
        source_dev = source % n_blk
        same_src = source_dev[:, None] == source_dev[None, :]
        earlier_src = source[None, :] < source[:, None]
        cell = jnp.sum((same_src & earlier_src).astype(jnp.int32), axis=1)
        return jnp.take(received, source_dev * capacity + cell, axis=0)

    return body


def solution(mesh):
    n_blk = mesh.shape["blk"]
    n_tp = mesh.shape["tp"]
    return jax.shard_map(
        make_body(n_blk, n_tp),
        mesh=mesh,
        in_specs=(
            P("blk", "tp"),
            P(),
            P(),
            P(),
            P(),
            P(None, None, "tp"),
            P("tp", None),
            P(),
            P(None, "tp"),
            P("tp", None),
            P(),
            P(None, "tp"),
        ),
        out_specs=P("blk", "tp"),
        check_vma=False,
    )
```

```python
import jax
import jax.numpy as jnp
from jax import lax
from jax.sharding import PartitionSpec as P

HDIM = 104


EPSILON = 1e-06
MASKED = -1e30
MAX_GROUPS = 125


def layer_norm(values, norm_gain):
    values = values.astype(jnp.float32)
    row_mean = jnp.mean(values, axis=-1, keepdims=True)
    centred = values - row_mean
    spread = jnp.mean(centred * centred, axis=-1, keepdims=True)
    return centred * lax.rsqrt(spread + EPSILON) * norm_gain


def segment_at(positions, request_ends):
    return jnp.sum((request_ends[None, :] <= (positions // 4)[:, None]).astype(jnp.int32), axis=1)


def tp_gather_rows(chunk, n_tp):
    me = lax.axis_index("tp")
    full = jnp.zeros((n_tp,) + chunk.shape, chunk.dtype)
    full = lax.dynamic_update_index_in_dim(full, chunk, me, 0)
    for step in range(1, n_tp):
        got = lax.ppermute(chunk, "tp", [(i, (i + step) % n_tp) for i in range(n_tp)])
        full = lax.dynamic_update_index_in_dim(full, got, (me - step) % n_tp, 0)
    return full


def tp_scatter_sum(partial, n_tp):
    me = lax.axis_index("tp")
    chunks = partial.reshape((n_tp, partial.shape[0] // n_tp) + partial.shape[1:])
    total = lax.dynamic_index_in_dim(chunks, me, 0, keepdims=False).astype(jnp.float32)
    for step in range(1, n_tp):
        send = lax.dynamic_index_in_dim(chunks, (me + step) % n_tp, 0, keepdims=False)
        got = lax.ppermute(send, "tp", [(i, (i + step) % n_tp) for i in range(n_tp)])
        total = total + got.astype(jnp.float32)
    return total


def tp_gather_rotated(chunk, n_tp):
    blocks = [chunk]
    for step in range(1, n_tp):
        blocks.append(lax.ppermute(chunk, "tp", [(i, (i + step) % n_tp) for i in range(n_tp)]))
    return jnp.concatenate(blocks, axis=0)


def tp_return_sum(partial, n_tp):
    rows = partial.shape[0] // n_tp
    total = partial[:rows].astype(jnp.float32)
    for step in range(1, n_tp):
        got = lax.ppermute(
            partial[step * rows : (step + 1) * rows],
            "tp",
            [(i, (i - step) % n_tp) for i in range(n_tp)],
        )
        total = total + got.astype(jnp.float32)
    return total


def make_body(n_blk, n_tp):
    def body(
        tokens,
        block_split,
        req_lengths,
        req_owners,
        norm1_gain,
        qkv_weight,
        out_weight,
        norm2_gain,
        up_weight,
        down_weight,
        merge_gain,
        merge_weight,
    ):
        tok_rows, width = tokens.shape
        half_rows = tok_rows // 2
        piece = half_rows // n_blk
        n_slots = block_split.shape[0]
        my_index = lax.axis_index("blk")

        slots = jnp.arange(n_slots, dtype=jnp.int32)
        inverse = jnp.sum(
            jnp.where(block_split[None, :] == slots[:, None], slots[None, :], 0), axis=1
        )
        spread = tokens.reshape(2, n_blk, piece, width).transpose(1, 0, 2, 3)
        spread = lax.all_to_all(spread, "blk", 0, 0, tiled=True)
        spread = spread.reshape(n_slots, piece, width)
        routed = jnp.take(spread, inverse, axis=0).reshape(n_blk, 1, 2, piece, width)
        routed = jnp.broadcast_to(routed, (n_blk, n_tp, 2, piece, width))
        routed = routed.reshape(n_blk * n_tp, 2, piece, width)
        routed = lax.all_to_all(routed, ("blk", "tp"), 0, 0, tiled=True)
        features = (
            routed.reshape(n_blk, n_tp, 2, piece, width)
            .transpose(2, 0, 3, 1, 4)
            .reshape(tok_rows, n_tp * width)
        )

        request_ends = jnp.cumsum(req_lengths).astype(jnp.int32)
        starts = request_ends - req_lengths
        row_base = my_index * tok_rows
        query_seg = segment_at(row_base + jnp.arange(tok_rows, dtype=jnp.int32), request_ends)
        key_pos = row_base - tok_rows + jnp.arange(3 * tok_rows, dtype=jnp.int32)
        key_valid = (key_pos >= 0) & (key_pos < n_blk * tok_rows)
        key_seg = jnp.where(key_valid, segment_at(key_pos, request_ends), -1)

        normed1 = layer_norm(features, norm1_gain).astype(jnp.bfloat16)
        projected = jnp.einsum(
            "td,dcf->ctf", normed1, qkv_weight, preferred_element_type=jnp.float32
        ).astype(jnp.bfloat16)
        queries = projected[0]
        key_value = projected[1:]
        from_prev = lax.ppermute(key_value, "blk", [(i, i + 1) for i in range(n_blk - 1)])
        from_next = lax.ppermute(key_value, "blk", [(i + 1, i) for i in range(n_blk - 1)])
        window = jnp.concatenate([from_prev, key_value, from_next], axis=1)

        head_count = qkv_weight.shape[2] // HDIM
        tp_index = lax.axis_index("tp")
        n_half = 2
        half_rows = tok_rows // n_half
        reach = 4 * MAX_GROUPS - 1
        key_span = min(3 * tok_rows, -(-(half_rows + 2 * reach) // 128) * 128)
        group_rows = tok_rows // 4
        out_width = merge_weight.shape[1]

        def one_half(part):
            row0 = part * half_rows
            key0 = min(row0, 3 * tok_rows - key_span)
            query_heads = queries[row0 : row0 + half_rows].reshape(half_rows, head_count, HDIM)
            seg_q = query_seg[row0 : row0 + half_rows]
            key_heads = window[0, key0 : key0 + key_span].reshape(key_span, head_count, HDIM)
            value_heads = window[1, key0 : key0 + key_span].reshape(key_span, head_count, HDIM)
            seg_k = key_seg[key0 : key0 + key_span]
            scores = jnp.einsum(
                "qhd,khd->hqk", query_heads, key_heads, preferred_element_type=jnp.float32
            ) * HDIM ** (-0.5)
            same_request = (seg_q[:, None] == seg_k[None, :])[None, :, :]
            scores = jnp.where(same_request, scores, MASKED)
            maxima = jnp.max(scores, axis=2)
            weights = jnp.where(same_request, jnp.exp(scores - maxima[:, :, None]), 0.0)
            totals = jnp.sum(weights, axis=2)
            mixed = jnp.einsum(
                "hqk,khd->qhd",
                weights.astype(jnp.bfloat16),
                value_heads,
                preferred_element_type=jnp.float32,
            )
            attended = (mixed / jnp.transpose(totals)[:, :, None]).reshape(half_rows, -1).astype(
                jnp.bfloat16
            )
            chunk_rows = half_rows // n_tp
            residual = lax.dynamic_slice_in_dim(
                features, row0 + tp_index * chunk_rows, chunk_rows, 0
            )
            ahead = (tp_index + jnp.arange(n_tp, dtype=jnp.int32)) % n_tp
            attended = jnp.take(
                attended.reshape(n_tp, chunk_rows, -1), ahead, axis=0
            ).reshape(half_rows, -1)
            partial = jnp.dot(attended, out_weight, preferred_element_type=jnp.float32).astype(
                jnp.bfloat16
            )
            total = partial[:chunk_rows].astype(jnp.float32)
            for step in range(1, n_tp):
                got = lax.ppermute(
                    partial[step * chunk_rows : (step + 1) * chunk_rows],
                    "tp",
                    [(i, (i + step) % n_tp) for i in range(n_tp)],
                )
                total = total + got.astype(jnp.float32)
            after_attention = residual.astype(jnp.float32) + total
            normed2 = layer_norm(after_attention, norm2_gain).astype(jnp.bfloat16)
            normed2 = tp_gather_rotated(normed2, n_tp)
            hidden = jax.nn.gelu(
                jnp.dot(normed2, up_weight, preferred_element_type=jnp.float32), approximate=False
            ).astype(jnp.bfloat16)
            after_mlp = after_attention + tp_return_sum(
                jnp.dot(hidden, down_weight, preferred_element_type=jnp.float32).astype(
                    jnp.bfloat16
                ),
                n_tp,
            )
            final_norm = layer_norm(after_mlp, merge_gain).astype(jnp.bfloat16)
            final_norm = tp_gather_rotated(final_norm, n_tp)
            half_groups = half_rows // 4
            grouped = final_norm.reshape(half_groups, 4 * final_norm.shape[1])
            merged = jnp.dot(grouped, merge_weight, preferred_element_type=jnp.float32).astype(
                jnp.bfloat16
            )
            rotated = merged.reshape(n_tp, half_groups // n_tp, out_width)
            back = (tp_index - jnp.arange(n_tp, dtype=jnp.int32)) % n_tp
            return jnp.take(rotated, back, axis=0).reshape(half_groups, out_width)

        merged = jnp.concatenate([one_half(part) for part in range(n_half)], axis=0)

        all_groups = jnp.arange(n_blk * group_rows, dtype=jnp.int32)
        position = jnp.arange(req_lengths.shape[0], dtype=jnp.int32)
        earlier = (req_owners[None, :] == req_owners[:, None]) & (position[None, :] < position[:, None])
        owner_offset = jnp.sum(jnp.where(earlier, req_lengths[None, :], 0), axis=1)
        shift = req_owners * group_rows + owner_offset - starts
        def target_of(groups):
            inside = (starts[None, :] <= groups[:, None]) & (groups[:, None] < request_ends[None, :])
            return jnp.sum(jnp.where(inside, shift[None, :], 0), axis=1) + groups

        target = target_of(all_groups)

        rounds = group_rows // n_blk
        spread_m = merged.reshape(rounds, n_blk, out_width).transpose(1, 0, 2)
        spread_m = lax.all_to_all(spread_m, "blk", 0, 0, tiled=True)
        spread_m = spread_m.reshape(n_blk * rounds, out_width)
        held_local = jnp.arange(n_blk * rounds, dtype=jnp.int32)
        held_group = (held_local // rounds) * group_rows + (held_local % rounds) * n_blk + my_index
        held_dest = target_of(held_group) // group_rows
        same_dest = held_dest[:, None] == held_dest[None, :]
        before = held_local[None, :] < held_local[:, None]
        held_rank = jnp.sum((same_dest & before).astype(jnp.int32), axis=1)
        capacity = 8
        dest_ids = jnp.arange(n_blk, dtype=jnp.int32)
        cells = jnp.arange(capacity, dtype=jnp.int32)
        hit = (held_dest[None, None, :] == dest_ids[:, None, None]) & (
            held_rank[None, None, :] == cells[None, :, None]
        )
        send_index = jnp.sum(jnp.where(hit, held_local[None, None, :], 0), axis=2)
        send = jnp.take(spread_m, send_index.reshape(-1), axis=0).reshape(n_blk, capacity, out_width)
        received = lax.all_to_all(send, "blk", 0, 0, tiled=True).reshape(n_blk * capacity, out_width)

        my_slots = my_index * group_rows + jnp.arange(group_rows, dtype=jnp.int32)
        source = jnp.sum(
            jnp.where(target[None, :] == my_slots[:, None], all_groups[None, :], 0), axis=1
        )
        source_dev = source % n_blk
        same_src = source_dev[:, None] == source_dev[None, :]
        earlier_src = source[None, :] < source[:, None]
        cell = jnp.sum((same_src & earlier_src).astype(jnp.int32), axis=1)
        return jnp.take(received, source_dev * capacity + cell, axis=0)

    return body


def solution(mesh):
    n_blk = mesh.shape["blk"]
    n_tp = mesh.shape["tp"]
    return jax.shard_map(
        make_body(n_blk, n_tp),
        mesh=mesh,
        in_specs=(
            P("blk", "tp"),
            P(),
            P(),
            P(),
            P(),
            P(None, None, "tp"),
            P("tp", None),
            P(),
            P(None, "tp"),
            P("tp", None),
            P(),
            P(None, "tp"),
        ),
        out_specs=P("blk", "tp"),
        check_vma=False,
    )
```
